32 devices in a mesh: blk: 16 (over z, x, core), rel: 2 (over y).
Axes of the slice: x: 2, y: 2, z: 4, core: 2. Of those that a mesh axis runs over, the one named last changes fastest.
Arguments:
- embeddings: float32 [65536, 200], P(('blk', 'rel')), may hold values from -1.8 to 1.8
- emb_state: float32 [65536], P(('blk', 'rel')), may hold values from 0.01 to 1
- operators: float32 [32, 200, 200], P('rel'), may hold values from -0.4375 to 0.4375
- op_state: float32 [32, 40000], P('rel', 'blk'), may hold values from 0.01 to 4
- requests: int32 [32, 8], P(('blk', 'rel')), may hold values from 0 to 31, as said below
- edge_src: int32 [32, 1024], P(('blk', 'rel')), may hold values from 0 to 2047
- edge_dst: int32 [32, 1024], P(('blk', 'rel')), may hold values from 0 to 2047
- negatives: int32 [32, 4, 1024], P(('blk', 'rel')), may hold values from 0 to 2047
Outputs:
- new_emb: float32 [65536, 200], P(('blk', 'rel'))
- new_emb_state: float32 [65536], P(('blk', 'rel'))
- new_operators: float32 [32, 200, 200], P('rel')
- new_op_state: float32 [32, 40000], P('rel', 'blk')
The draws below stay inside these ranges and needn't reach their ends.
Inputs may be any that keep to these rules, and one draw needn't show every extreme that they name: `requests`: the 8 relations of one bucket are distinct. Call r // 16 the owner of relation r: at most 4 of one bucket's relations have the same owner, and in every bucket exactly 4 share one owner.
All inputs are finite; a program needn't handle non-finite values.
Results may differ from the reference program's by a relative error of at most 0.0018.
The reference program's roundings to bfloat16 on the way (of `emb_bf`, `op_bf`, `trans_bf`, `weights` and `g_bf`) count: a program that leaves them out, or rounds other values in their place, can miss the bound.
Values may be sent and summed in bfloat16 or wider, within the bound.
No kernel may reach another device: no remote copies, remote signals or barrier semaphores. Data moves between devices by JAX's collectives and lax.ppermute only.
A program may use at most 128 MiB of HBM per device.

```python
import math
import jax
import jax.numpy as jnp
from jax import lax

D = 200
ENT_DEV = 2048
REL_DEV = 16
REQ = 8
GROUP = 128
SPANS = 4
NEG = 1024
PARTS_SIZE = 32
ENTITIES = 65536
NREL = 32
EDGES = 1024
SPAN = 256
CAP = 4
N_REL = 2


def draw_requests(key, part):
    keys = jax.random.split(key, 5)
    first = jax.random.randint(keys[0], (PARTS_SIZE,), 0, N_REL)
    second = jax.random.randint(keys[1], (PARTS_SIZE,), 0, N_REL)
    third = jax.random.randint(keys[2], (PARTS_SIZE,), 0, N_REL)
    hot_owner = jnp.minimum(jnp.minimum(first, second), third)
    offsets = jax.random.randint(keys[3], (PARTS_SIZE,), 0, max(N_REL - 1, 1))
    slots = jnp.arange(REQ, dtype=jnp.int32)
    others = (hot_owner[:, None] + 1 + (offsets[:, None] + slots[None, :]) % max(N_REL - 1, 1)) % N_REL
    owner_ids = jnp.where(slots[None, :] < CAP, hot_owner[:, None], others)
    row_keys = jax.random.split(keys[4], PARTS_SIZE)
    local_ids = jax.vmap(lambda row_key: jax.random.permutation(row_key, REL_DEV)[:REQ])(row_keys)
    return (owner_ids * REL_DEV + local_ids).astype(jnp.int32)


def plant(result, rng, least, largest):
    shape = result.shape
    index_at = [jax.random.randint(jax.random.fold_in(rng, axis), (), 0, shape[axis]) for axis in range(len(shape))]
    result = result.at[tuple(index_at)].set(least)
    longest = shape.index(max(shape))
    index_at[longest] = (index_at[longest] + 1) % shape[longest]
    return result.at[tuple(index_at)].set(largest)


def shard_levels(own_key, extent, cuts, low, largest):
    factor_of = 1.0
    for position, blocks in cuts:
        draws = jax.random.uniform(jax.random.fold_in(jax.random.fold_in(own_key, 6), position), (blocks,), jnp.float32, low / len(cuts), largest / len(cuts))
        factor_of = factor_of * jnp.repeat(jnp.exp(draws), extent[position] // blocks).reshape((-1,) + (1,) * (len(extent) - 1 - position))
    return factor_of


def gaussian(own_key, shape, scale, limit, cuts=(), kind=jnp.bfloat16):
    drawn = jax.random.normal(own_key, shape, jnp.float32) * scale
    if len(cuts) > 0:
        drawn = shard_levels(own_key, shape, cuts, -0.22, 0.18) * drawn
    return jnp.clip(drawn, min=-limit, max=limit).astype(kind)


def setup_inputs(seed: int = 0) -> dict:
    key_of = jax.random.split(jax.random.key(seed), 9)
    return {
        "embeddings": gaussian(key_of[0], (ENTITIES, D), 0.3, 1.8, ((0, 32),), jnp.float32),
        "emb_state": jnp.clip(jnp.exp(math.log(1.0) - 4.6051702 * jax.random.uniform(key_of[1], (ENTITIES,), jnp.float32) ** shard_levels(key_of[1], (ENTITIES,), ((0, 32),), -0.2, 0.2)), 0.01, 1.0),
        "operators": gaussian(key_of[2], (NREL, D, D), D ** -0.5, 0.4375, ((0, 2),), jnp.float32),
        "op_state": jnp.clip(jnp.exp(math.log(4.0) - 5.9914646 * jax.random.uniform(key_of[3], (NREL, D * D), jnp.float32) ** shard_levels(key_of[3], (NREL, D * D), ((0, 2), (1, 16)), -0.2, 0.2)), 0.01, 4.0),
        "requests": draw_requests(jax.random.fold_in(key_of[8], 71), 0),
        "edge_src": plant(jax.random.randint(key_of[5], (PARTS_SIZE, EDGES), 0, ENT_DEV), jax.random.fold_in(key_of[5], 1), 0, ENT_DEV - 1).astype(jnp.int32),
        "edge_dst": plant(jax.random.randint(key_of[6], (PARTS_SIZE, EDGES), 0, ENT_DEV), jax.random.fold_in(key_of[6], 1), 0, ENT_DEV - 1).astype(jnp.int32),
        "negatives": plant(jax.random.randint(key_of[7], (PARTS_SIZE, SPANS, NEG), 0, ENT_DEV), jax.random.fold_in(key_of[7], 1), 0, ENT_DEV - 1).astype(jnp.int32),
    }


def bucket_grads(src_block, dst_block, operator_rows, src_ids, dst_ids, neg_ids):
    src_rows = jnp.take(src_block, src_ids, axis=0).reshape(REQ, GROUP, D)
    dst_rows = jnp.take(dst_block, dst_ids, axis=0)
    transformed = jnp.einsum('ked,kgd->kge', operator_rows.astype(jnp.float32), src_rows.astype(jnp.float32)).reshape(EDGES, D)
    trans_bf = transformed.astype(jnp.bfloat16)
    positive = lax.optimization_barrier(jnp.sum(transformed * dst_rows.astype(jnp.float32), axis=1))
    pos_grad = -jax.nn.sigmoid(-positive)
    neg_scale = 1.0 / jnp.sqrt(jnp.float32(NEG))
    dst_grad = jax.ops.segment_sum(pos_grad[:, None] * transformed, dst_ids, ENT_DEV)
    pieces = []
    for span_id in range(SPANS):
        neg_rows = jnp.take(dst_block, neg_ids[span_id], axis=0)
        edge_rows = trans_bf[span_id * SPAN:(span_id + 1) * SPAN]
        scores = jnp.dot(edge_rows, neg_rows.T, preferred_element_type=jnp.float32)
        weights = (jax.nn.sigmoid(scores) * neg_scale).astype(jnp.bfloat16)
        pieces.append(jnp.dot(weights, neg_rows, preferred_element_type=jnp.float32))
        neg_grad = jnp.dot(weights.T, edge_rows, preferred_element_type=jnp.float32)
        dst_grad = dst_grad + jax.ops.segment_sum(neg_grad, neg_ids[span_id], ENT_DEV)
    g_trans = pos_grad[:, None] * dst_rows.astype(jnp.float32) + jnp.concatenate(pieces, axis=0)
    g_bf = g_trans.astype(jnp.bfloat16).reshape(REQ, GROUP, D)
    src_terms = jnp.einsum('ked,kge->kgd', operator_rows.astype(jnp.float32), g_bf.astype(jnp.float32)).reshape(EDGES, D)
    src_grad = jax.ops.segment_sum(src_terms, src_ids, ENT_DEV)
    op_grad = jnp.einsum('kge,kgd->ked', g_bf.astype(jnp.float32), src_rows.astype(jnp.float32))
    return (src_grad, dst_grad, op_grad)

def reference(embeddings, emb_state, operators, op_state, requests, edge_src, edge_dst, negatives):
    emb_bf = embeddings.astype(jnp.bfloat16).reshape(PARTS_SIZE, ENT_DEV, D)
    dst_blocks = jnp.roll(emb_bf, N_REL, axis=0)
    op_bf = operators.astype(jnp.bfloat16)

    def one_bucket(inputs):
        src_block, dst_block, request_row, src_ids, dst_ids, neg_ids = inputs
        operator_rows = jnp.take(op_bf, request_row, axis=0)
        return bucket_grads(src_block, dst_block, operator_rows, src_ids, dst_ids, neg_ids)
    src_grads, dst_grads, op_grads = lax.map(one_bucket, (emb_bf, dst_blocks, requests, edge_src, edge_dst, negatives))
    entity_grad = (src_grads + jnp.roll(dst_grads, -N_REL, axis=0)).reshape(ENTITIES, D)
    new_emb_state = emb_state + lax.optimization_barrier(jnp.mean(entity_grad * entity_grad, axis=1))
    new_emb = embeddings - 0.3 * entity_grad / (jnp.sqrt(new_emb_state)[:, None] + 1e-10)
    op_total = jax.ops.segment_sum(op_grads.reshape(PARTS_SIZE * REQ, D * D), requests.reshape(-1), NREL)
    new_op_state = op_state + op_total * op_total
    new_ops = operators.reshape(NREL, D * D) - 0.3 * op_total / (jnp.sqrt(new_op_state) + 1e-10)
    return (new_emb, new_emb_state, new_ops.reshape(NREL, D, D), new_op_state)
```

```python
import jax
import jax.numpy as jnp
from jax import lax
from jax.sharding import PartitionSpec as P


def shifted(value, axis, by):
    count = lax.axis_size(axis)
    return lax.ppermute(value, axis, [(i, (i + by) % count) for i in range(count)])


def flipped(value, axis, bit):
    count = lax.axis_size(axis)
    return lax.ppermute(value, axis, [(i, i ^ (1 << bit)) for i in range(count)])


def bit_at(index, bit):
    return (index // (1 << bit)) % 2


def exchange(rows, axis):
    count = lax.axis_size(axis)
    if count != 2:
        return lax.all_to_all(rows, axis, split_axis=0, concat_axis=0, tiled=True)
    me = lax.axis_index(axis)
    mine = lax.dynamic_index_in_dim(rows, me, 0, keepdims=False)
    other = lax.dynamic_index_in_dim(rows, 1 - me, 0, keepdims=False)
    got = flipped(other, axis, 0)
    first = jnp.where(me == 0, mine, got)
    second = jnp.where(me == 0, got, mine)
    return jnp.stack([first, second], axis=0)


def scatter_rows(onehot, values):
    return lax.dot_general(
        onehot,
        values,
        (((0,), (0,)), ((), ())),
        precision=lax.Precision.HIGHEST,
        preferred_element_type=jnp.float32,
    )


def halving_sum(rows, axis):
    count = lax.axis_size(axis)
    bits = count.bit_length() - 1
    me = lax.axis_index(axis)
    height, width = rows.shape
    share = width // count
    cur = rows.reshape((height,) + (2,) * bits + (share,))
    for bit in range(bits):
        mine = bit_at(me, bit)
        keep = lax.dynamic_index_in_dim(cur, mine, cur.ndim - 2, keepdims=False)
        send = lax.dynamic_index_in_dim(cur, 1 - mine, cur.ndim - 2, keepdims=False)
        cur = keep + flipped(send, axis, bit)
    return cur


def doubling_gather(share_rows, axis):
    count = lax.axis_size(axis)
    bits = count.bit_length() - 1
    me = lax.axis_index(axis)
    height, share = share_rows.shape
    cur = share_rows
    for bit in reversed(range(bits)):
        got = flipped(cur, axis, bit)
        low = bit_at(me, bit) == 0
        cur = jnp.stack([jnp.where(low, cur, got), jnp.where(low, got, cur)], axis=cur.ndim - 1)
    return cur.reshape(height, count * share)


def shards(embeddings, emb_state, operators, op_state, requests, edge_src, edge_dst, negatives):
    rel_count = lax.axis_size("rel")
    blk_count = lax.axis_size("blk")
    ent_rows, feature_count = embeddings.shape
    rel_local = operators.shape[0]
    req_count = requests.shape[1]
    capacity = max(req_count // 4, req_count // rel_count)
    slot_count = rel_count * capacity
    edge_count = edge_src.shape[1]
    group_size = edge_count // req_count
    span_count = negatives.shape[1]
    neg_count = negatives.shape[2]
    span_size = edge_count // span_count
    emb_bf = embeddings.astype(jnp.bfloat16)
    dst_block = shifted(emb_bf, "blk", 1)
    request_ids = requests[0]
    owner_ids = request_ids // rel_local
    local_ids = request_ids % rel_local
    owner_hot = (owner_ids[:, None] == jnp.arange(rel_count, dtype=jnp.int32)[None, :]).astype(
        jnp.int32
    )
    rank_ids = jnp.sum((jnp.cumsum(owner_hot, axis=0) - 1) * owner_hot, axis=1)
    slot_of = owner_ids * capacity + rank_ids
    slot_hit = slot_of[:, None] == jnp.arange(slot_count, dtype=jnp.int32)[None, :]
    slot_valid = jnp.any(slot_hit, axis=0)
    req_of_slot = jnp.sum(
        jnp.where(slot_hit, jnp.arange(req_count, dtype=jnp.int32)[:, None], 0), axis=0
    )
    wanted = jnp.where(
        slot_valid, jnp.take(local_ids, req_of_slot), -1
    ).reshape(rel_count, capacity)
    asked = exchange(wanted, "rel")
    asked_flat = asked.reshape(-1)
    op_bf = operators.astype(jnp.bfloat16)
    served = jnp.take(op_bf, jnp.maximum(asked_flat, 0), axis=0).reshape(
        rel_count, capacity, feature_count, feature_count
    )
    fetched = exchange(served, "rel").reshape(slot_count, feature_count, feature_count)
    my_ops = jnp.take(fetched, slot_of, axis=0)
    entity_cols = jnp.arange(ent_rows, dtype=jnp.int32)
    src_ids = edge_src[0]
    dst_ids = edge_dst[0]
    src_match = src_ids[:, None] == entity_cols[None, :]
    dst_match = dst_ids[:, None] == entity_cols[None, :]
    src_rows = (
        jnp.dot(src_match.astype(jnp.bfloat16), emb_bf, preferred_element_type=jnp.float32)
        .astype(jnp.bfloat16)
        .reshape(req_count, group_size, feature_count)
    )
    dst_rows = jnp.dot(
        dst_match.astype(jnp.bfloat16), dst_block, preferred_element_type=jnp.float32
    ).astype(jnp.bfloat16)
    transformed = jnp.einsum(
        "ked,kgd->kge", my_ops, src_rows, preferred_element_type=jnp.float32
    ).reshape(edge_count, feature_count)
    trans_bf = transformed.astype(jnp.bfloat16)
    positive = jnp.sum(transformed * dst_rows.astype(jnp.float32), axis=1)
    pos_grad = -jax.nn.sigmoid(-positive)
    neg_scale = 1.0 / jnp.sqrt(jnp.float32(neg_count))
    block_grad = scatter_rows(dst_match.astype(jnp.float32), pos_grad[:, None] * transformed)
    pieces = []
    for span_id in range(span_count):
        neg_match = negatives[0, span_id][:, None] == entity_cols[None, :]
        neg_rows = jnp.dot(
            neg_match.astype(jnp.bfloat16), dst_block, preferred_element_type=jnp.float32
        ).astype(jnp.bfloat16)
        edge_rows = trans_bf[span_id * span_size : (span_id + 1) * span_size]
        scores = jnp.dot(edge_rows, neg_rows.T, preferred_element_type=jnp.float32)
        weights = (jax.nn.sigmoid(scores) * neg_scale).astype(jnp.bfloat16)
        pieces.append(jnp.dot(weights, neg_rows, preferred_element_type=jnp.float32))
        neg_grad = jnp.dot(weights.T, edge_rows, preferred_element_type=jnp.float32)
        block_grad = block_grad + scatter_rows(neg_match.astype(jnp.float32), neg_grad)
    g_trans = pos_grad[:, None] * dst_rows.astype(jnp.float32) + jnp.concatenate(pieces, axis=0)
    g_bf = g_trans.astype(jnp.bfloat16).reshape(req_count, group_size, feature_count)
    src_terms = jnp.einsum(
        "ked,kge->kgd", my_ops, g_bf, preferred_element_type=jnp.float32
    ).reshape(edge_count, feature_count)
    src_grad = scatter_rows(src_match.astype(jnp.float32), src_terms)
    returned = shifted(block_grad, "blk", -1)
    entity_grad = src_grad + returned
    new_emb_state = emb_state + jnp.mean(entity_grad * entity_grad, axis=1)
    new_emb = embeddings - 0.3 * entity_grad / (jnp.sqrt(new_emb_state)[:, None] + 1e-10)
    flat_size = feature_count * feature_count
    slot_live = slot_valid.astype(jnp.bfloat16)[:, None, None]
    g_slots = jnp.take(g_bf, req_of_slot, axis=0) * slot_live
    src_slots = jnp.take(src_rows, req_of_slot, axis=0)
    outgoing = jnp.einsum(
        "kge,kgd->ked", g_slots, src_slots, preferred_element_type=jnp.float32
    ).reshape(rel_count, capacity, flat_size)
    incoming = exchange(outgoing, "rel").reshape(slot_count, flat_size)
    owner_match = (
        asked_flat[:, None] == jnp.arange(rel_local, dtype=jnp.int32)[None, :]
    ).astype(jnp.float32)
    owned_grad = scatter_rows(owner_match, incoming)
    share_size = op_state.shape[1]
    summed = halving_sum(owned_grad, "blk")
    op_share = lax.dynamic_index_in_dim(
        operators.reshape(rel_local, blk_count, share_size), lax.axis_index("blk"), 1, keepdims=False
    )
    state_next = op_state + summed * summed
    updated = op_share - 0.3 * summed / (jnp.sqrt(state_next) + 1e-10)
    new_ops = doubling_gather(updated, "blk")
    return (
        new_emb,
        new_emb_state,
        new_ops.reshape(rel_local, feature_count, feature_count),
        state_next,
    )


def solution(mesh):
    placed = (
        P(("blk", "rel"), None),
        P(("blk", "rel")),
        P("rel", None, None),
        P("rel", "blk"),
        P(("blk", "rel"), None),
        P(("blk", "rel"), None),
        P(("blk", "rel"), None),
        P(("blk", "rel"), None, None),
    )
    return jax.shard_map(
        shards,
        mesh=mesh,
        in_specs=placed,
        out_specs=(
            P(("blk", "rel"), None),
            P(("blk", "rel")),
            P("rel", None, None),
            P("rel", "blk"),
        ),
        check_vma=False,
    )
```

```python
import jax
import jax.numpy as jnp
from jax import lax
from jax.sharding import PartitionSpec as P


def shifted(value, axis, by):
    count = lax.axis_size(axis)
    return lax.ppermute(value, axis, [(i, (i + by) % count) for i in range(count)])


def flipped(value, axis, bit):
    count = lax.axis_size(axis)
    return lax.ppermute(value, axis, [(i, i ^ (1 << bit)) for i in range(count)])


def chip_hop(value, axis, offset):
    count = lax.axis_size(axis)
    chips = count // 2
    return lax.ppermute(
        value, axis, [(i, ((i // 2 + offset) % chips) * 2 + i % 2) for i in range(count)]
    )


def exchange(rows, axis):
    return lax.all_to_all(rows, axis, split_axis=0, concat_axis=0, tiled=True)


def scatter_rows(onehot, values):
    return lax.dot_general(
        onehot,
        values,
        (((0,), (0,)), ((), ())),
        precision=lax.Precision.HIGHEST,
        preferred_element_type=jnp.float32,
    )


def scatter_split(onehot_bf, values):
    width = values.shape[1]
    high = values.astype(jnp.bfloat16)
    low = (values - high.astype(jnp.float32)).astype(jnp.bfloat16)
    both = lax.dot_general(
        onehot_bf,
        jnp.concatenate([high, low], axis=1),
        (((0,), (0,)), ((), ())),
        preferred_element_type=jnp.float32,
    )
    return both[:, :width] + both[:, width:]


def pick_rows(slots, index, valid):
    picked = jnp.take(slots, jnp.maximum(index, 0), axis=0)
    return jnp.where(valid.reshape((-1,) + (1,) * (slots.ndim - 1)), picked, 0.0)


def owner_sum(own_dense, axis):
    count = lax.axis_size(axis)
    chips = count // 2
    me = lax.axis_index(axis)
    core = me % 2
    chip = me // 2
    height, width = own_dense.shape
    share = width // count
    cur = own_dense.reshape(height, chips, 2, share)
    keep = lax.dynamic_index_in_dim(cur, core, 2, keepdims=False)
    send = lax.dynamic_index_in_dim(cur, 1 - core, 2, keepdims=False)
    got = flipped(send, axis, 0)
    half = keep + got
    total = lax.dynamic_index_in_dim(half, chip, 1, keepdims=False)
    for offset in range(1, chips):
        part = lax.dynamic_index_in_dim(half, (chip + offset) % chips, 1, keepdims=False)
        total = total + chip_hop(part, axis, offset)
    return total


def owner_gather(share_rows, axis):
    count = lax.axis_size(axis)
    chips = count // 2
    me = lax.axis_index(axis)
    core = me % 2
    chip = me // 2
    height, share = share_rows.shape
    pieces = [share_rows]
    for offset in range(1, chips):
        pieces.append(chip_hop(share_rows, axis, chips - offset))
    stacked = jnp.stack(pieces, axis=1)
    order = (jnp.arange(chips, dtype=jnp.int32) - chip) % chips
    mine = jnp.take(stacked, order, axis=1)
    theirs = flipped(mine, axis, 0)
    low = core == 0
    full = jnp.stack([jnp.where(low, mine, theirs), jnp.where(low, theirs, mine)], axis=2)
    return full.reshape(height, count * share)


def shards(embeddings, emb_state, operators, op_state, requests, edge_src, edge_dst, negatives):
    rel_count = lax.axis_size("rel")
    ent_rows, feature_count = embeddings.shape
    rel_local = operators.shape[0]
    req_count = requests.shape[1]
    capacity = max(req_count // 4, req_count // rel_count)
    slot_count = rel_count * capacity
    edge_count = edge_src.shape[1]
    group_size = edge_count // req_count
    span_count = negatives.shape[1]
    neg_count = negatives.shape[2]
    span_size = edge_count // span_count
    flat_size = feature_count * feature_count
    emb_bf = embeddings.astype(jnp.bfloat16)
    dst_block = shifted(emb_bf, "blk", 1)
    request_ids = requests[0]
    owner_ids = request_ids // rel_local
    local_ids = request_ids % rel_local
    owner_hot = (owner_ids[:, None] == jnp.arange(rel_count, dtype=jnp.int32)[None, :]).astype(
        jnp.int32
    )
    rank_ids = jnp.sum((jnp.cumsum(owner_hot, axis=0) - 1) * owner_hot, axis=1)
    slot_of = owner_ids * capacity + rank_ids
    slot_hit = slot_of[:, None] == jnp.arange(slot_count, dtype=jnp.int32)[None, :]
    slot_valid = jnp.any(slot_hit, axis=0)
    req_of_slot = jnp.sum(
        jnp.where(slot_hit, jnp.arange(req_count, dtype=jnp.int32)[:, None], 0), axis=0
    )
    wanted = jnp.where(slot_valid, jnp.take(local_ids, req_of_slot), -1).reshape(
        rel_count, capacity
    )
    op_bf = operators.astype(jnp.bfloat16)
    rel_me = lax.axis_index("rel")
    if rel_count == 2:
        partner_asks = flipped(lax.dynamic_index_in_dim(wanted, 1 - rel_me, 0, keepdims=False), "rel", 0)
        own_asks = lax.dynamic_index_in_dim(wanted, rel_me, 0, keepdims=False)
        served = jnp.take(op_bf, jnp.maximum(partner_asks, 0), axis=0)
        got_ops = flipped(served, "rel", 0)
        own_ops = jnp.take(op_bf, jnp.maximum(own_asks, 0), axis=0)
        both_ops = jnp.concatenate([own_ops, got_ops], axis=0)
        my_ops = jnp.take(both_ops, jnp.where(owner_ids == rel_me, 0, capacity) + rank_ids, axis=0)
    else:
        asked = exchange(wanted, "rel")
        asked_flat = asked.reshape(-1)
        served = jnp.take(op_bf, jnp.maximum(asked_flat, 0), axis=0).reshape(
            rel_count, capacity, feature_count, feature_count
        )
        fetched = exchange(served, "rel").reshape(slot_count, feature_count, feature_count)
        my_ops = jnp.take(fetched, slot_of, axis=0)
    entity_cols = jnp.arange(ent_rows, dtype=jnp.int32)
    src_ids = edge_src[0]
    dst_ids = edge_dst[0]
    src_match = (src_ids[:, None] == entity_cols[None, :]).astype(jnp.bfloat16)
    dst_match = (dst_ids[:, None] == entity_cols[None, :]).astype(jnp.bfloat16)
    src_rows = (
        jnp.dot(src_match, emb_bf, preferred_element_type=jnp.float32)
        .astype(jnp.bfloat16)
        .reshape(req_count, group_size, feature_count)
    )
    dst_rows = jnp.dot(dst_match, dst_block, preferred_element_type=jnp.float32).astype(jnp.bfloat16)
    transformed = jnp.einsum(
        "ked,kgd->kge", my_ops, src_rows, preferred_element_type=jnp.float32
    ).reshape(edge_count, feature_count)
    trans_bf = transformed.astype(jnp.bfloat16)
    positive = jnp.sum(transformed * dst_rows.astype(jnp.float32), axis=1)
    pos_grad = -jax.nn.sigmoid(-positive)
    neg_scale = 1.0 / jnp.sqrt(jnp.float32(neg_count))
    block_terms = [pos_grad[:, None] * transformed]
    block_hits = [dst_match]
    pieces = []
    for span_id in range(span_count):
        neg_match = (negatives[0, span_id][:, None] == entity_cols[None, :]).astype(jnp.bfloat16)
        neg_rows = jnp.dot(neg_match, dst_block, preferred_element_type=jnp.float32).astype(
            jnp.bfloat16
        )
        edge_rows = trans_bf[span_id * span_size : (span_id + 1) * span_size]
        scores = jnp.dot(edge_rows, neg_rows.T, preferred_element_type=jnp.float32)
        weights = (jax.nn.sigmoid(scores) * neg_scale).astype(jnp.bfloat16)
        pieces.append(jnp.dot(weights, neg_rows, preferred_element_type=jnp.float32))
        block_terms.append(jnp.dot(weights.T, edge_rows, preferred_element_type=jnp.float32))
        block_hits.append(neg_match)
    g_trans = pos_grad[:, None] * dst_rows.astype(jnp.float32) + jnp.concatenate(pieces, axis=0)
    g_bf = g_trans.astype(jnp.bfloat16).reshape(req_count, group_size, feature_count)
    req_grads = jnp.einsum(
        "kge,kgd->ked", g_bf, src_rows, preferred_element_type=jnp.float32
    ).reshape(req_count, flat_size)
    blk_count = lax.axis_size("blk")
    share_size = op_state.shape[1]
    rel_cols = jnp.arange(rel_local, dtype=jnp.int32)
    if rel_count == 2:
        partner_slots = req_of_slot.reshape(rel_count, capacity)
        partner_valid = slot_valid.reshape(rel_count, capacity)
        to_partner = pick_rows(
            req_grads,
            lax.dynamic_index_in_dim(partner_slots, 1 - rel_me, 0, keepdims=False),
            lax.dynamic_index_in_dim(partner_valid, 1 - rel_me, 0, keepdims=False),
        )
        from_partner = flipped(to_partner, "rel", 0)
        mine_hit = (owner_ids == rel_me)[:, None] & (local_ids[:, None] == rel_cols[None, :])
        own_dense = pick_rows(
            req_grads,
            jnp.sum(jnp.where(mine_hit, jnp.arange(req_count, dtype=jnp.int32)[:, None], 0), axis=0),
            jnp.any(mine_hit, axis=0),
        )
        their_hit = partner_asks[:, None] == rel_cols[None, :]
        their_index = jnp.sum(
            jnp.where(their_hit, jnp.arange(capacity, dtype=jnp.int32)[:, None], 0), axis=0
        )
        their_valid = jnp.any(their_hit, axis=0)
        summed = owner_sum(own_dense + pick_rows(from_partner, their_index, their_valid), "blk")
    else:
        outgoing = pick_rows(req_grads, req_of_slot, slot_valid).reshape(
            rel_count, capacity, flat_size
        )
        incoming = exchange(outgoing, "rel").reshape(slot_count, flat_size)
        owner_match = (asked_flat[:, None] == rel_cols[None, :]).astype(jnp.float32)
        summed = owner_sum(scatter_rows(owner_match, incoming), "blk")
    src_terms = jnp.einsum(
        "ked,kge->kgd", my_ops, g_bf, preferred_element_type=jnp.float32
    ).reshape(edge_count, feature_count)
    src_grad = scatter_split(src_match, src_terms)
    block_grad = scatter_split(
        jnp.concatenate(block_hits, axis=0), jnp.concatenate(block_terms, axis=0)
    )
    returned = shifted(block_grad, "blk", -1)
    entity_grad = src_grad + returned
    new_emb_state = emb_state + jnp.mean(entity_grad * entity_grad, axis=1)
    new_emb = embeddings - 0.3 * entity_grad / (jnp.sqrt(new_emb_state)[:, None] + 1e-10)
    op_share = lax.dynamic_index_in_dim(
        operators.reshape(rel_local, blk_count, share_size), lax.axis_index("blk"), 1, keepdims=False
    )
    state_next = op_state + summed * summed
    updated = op_share - 0.3 * summed / (jnp.sqrt(state_next) + 1e-10)
    new_ops = owner_gather(updated, "blk")
    return (
        new_emb,
        new_emb_state,
        new_ops.reshape(rel_local, feature_count, feature_count),
        state_next,
    )


def solution(mesh):
    placed = (
        P(("blk", "rel"), None),
        P(("blk", "rel")),
        P("rel", None, None),
        P("rel", "blk"),
        P(("blk", "rel"), None),
        P(("blk", "rel"), None),
        P(("blk", "rel"), None),
        P(("blk", "rel"), None, None),
    )
    return jax.shard_map(
        shards,
        mesh=mesh,
        in_specs=placed,
        out_specs=(
            P(("blk", "rel"), None),
            P(("blk", "rel")),
            P("rel", None, None),
            P("rel", "blk"),
        ),
        check_vma=False,
    )
```

```python
import jax
import jax.numpy as jnp
from jax import lax
from jax.sharding import PartitionSpec as P


def shifted(value, axis, by):
    count = lax.axis_size(axis)
    return lax.ppermute(value, axis, [(i, (i + by) % count) for i in range(count)])


def flipped(value, axis, bit):
    count = lax.axis_size(axis)
    return lax.ppermute(value, axis, [(i, i ^ (1 << bit)) for i in range(count)])


def chip_hop(value, axis, offset):
    count = lax.axis_size(axis)
    chips = count // 2
    return lax.ppermute(
        value, axis, [(i, ((i // 2 + offset) % chips) * 2 + i % 2) for i in range(count)]
    )


def exchange(rows, axis):
    return lax.all_to_all(rows, axis, split_axis=0, concat_axis=0, tiled=True)


def scatter_rows(onehot, values):
    return lax.dot_general(
        onehot,
        values,
        (((0,), (0,)), ((), ())),
        precision=lax.Precision.HIGHEST,
        preferred_element_type=jnp.float32,
    )


def pick_rows(slots, index, valid):
    picked = jnp.take(slots, jnp.maximum(index, 0), axis=0)
    return jnp.where(valid.reshape((-1,) + (1,) * (slots.ndim - 1)), picked, 0.0)


def owner_sum(own_dense, axis, riders):
    count = lax.axis_size(axis)
    chips = count // 2
    me = lax.axis_index(axis)
    core = me % 2
    chip = me // 2
    height, width = own_dense.shape
    share = width // count
    cur = own_dense.reshape(height, chips, 2, share)
    keep = lax.dynamic_index_in_dim(cur, core, 2, keepdims=False)
    send = lax.dynamic_index_in_dim(cur, 1 - core, 2, keepdims=False)
    got = flipped(send, axis, 0)
    half, riders = lax.optimization_barrier((keep + got, riders))
    total = lax.dynamic_index_in_dim(half, chip, 1, keepdims=False)
    for offset in range(1, chips):
        part = lax.dynamic_index_in_dim(half, (chip + offset) % chips, 1, keepdims=False)
        total = total + chip_hop(part, axis, offset)
    return total, riders


def owner_gather(share_rows, axis):
    count = lax.axis_size(axis)
    chips = count // 2
    me = lax.axis_index(axis)
    core = me % 2
    chip = me // 2
    height, share = share_rows.shape
    pieces = [share_rows]
    for offset in range(1, chips):
        pieces.append(chip_hop(share_rows, axis, chips - offset))
    stacked = jnp.stack(pieces, axis=1)
    order = (jnp.arange(chips, dtype=jnp.int32) - chip) % chips
    mine = jnp.take(stacked, order, axis=1)
    theirs = flipped(mine, axis, 0)
    low = core == 0
    full = jnp.stack([jnp.where(low, mine, theirs), jnp.where(low, theirs, mine)], axis=2)
    return full.reshape(height, count * share)


def shards(embeddings, emb_state, operators, op_state, requests, edge_src, edge_dst, negatives):
    rel_count = lax.axis_size("rel")
    ent_rows, feature_count = embeddings.shape
    rel_local = operators.shape[0]
    req_count = requests.shape[1]
    capacity = max(req_count // 4, req_count // rel_count)
    slot_count = rel_count * capacity
    edge_count = edge_src.shape[1]
    group_size = edge_count // req_count
    span_count = negatives.shape[1]
    neg_count = negatives.shape[2]
    span_size = edge_count // span_count
    flat_size = feature_count * feature_count
    emb_bf = embeddings.astype(jnp.bfloat16)
    dst_block = shifted(emb_bf, "blk", 1)
    request_ids = requests[0]
    owner_ids = request_ids // rel_local
    local_ids = request_ids % rel_local
    owner_hot = (owner_ids[:, None] == jnp.arange(rel_count, dtype=jnp.int32)[None, :]).astype(
        jnp.int32
    )
    rank_ids = jnp.sum((jnp.cumsum(owner_hot, axis=0) - 1) * owner_hot, axis=1)
    slot_of = owner_ids * capacity + rank_ids
    slot_hit = slot_of[:, None] == jnp.arange(slot_count, dtype=jnp.int32)[None, :]
    slot_valid = jnp.any(slot_hit, axis=0)
    req_of_slot = jnp.sum(
        jnp.where(slot_hit, jnp.arange(req_count, dtype=jnp.int32)[:, None], 0), axis=0
    )
    wanted = jnp.where(slot_valid, jnp.take(local_ids, req_of_slot), -1).reshape(
        rel_count, capacity
    )
    op_bf = operators.astype(jnp.bfloat16)
    rel_me = lax.axis_index("rel")
    if rel_count == 2:
        partner_asks = flipped(lax.dynamic_index_in_dim(wanted, 1 - rel_me, 0, keepdims=False), "rel", 0)
        own_asks = lax.dynamic_index_in_dim(wanted, rel_me, 0, keepdims=False)
        served = jnp.take(op_bf, jnp.maximum(partner_asks, 0), axis=0)
        got_ops = flipped(served, "rel", 0)
        own_ops = jnp.take(op_bf, jnp.maximum(own_asks, 0), axis=0)
        both_ops = jnp.concatenate([own_ops, got_ops], axis=0)
        my_ops = jnp.take(both_ops, jnp.where(owner_ids == rel_me, 0, capacity) + rank_ids, axis=0)
    else:
        asked = exchange(wanted, "rel")
        asked_flat = asked.reshape(-1)
        served = jnp.take(op_bf, jnp.maximum(asked_flat, 0), axis=0).reshape(
            rel_count, capacity, feature_count, feature_count
        )
        fetched = exchange(served, "rel").reshape(slot_count, feature_count, feature_count)
        my_ops = jnp.take(fetched, slot_of, axis=0)
    entity_cols = jnp.arange(ent_rows, dtype=jnp.int32)
    src_ids = edge_src[0]
    dst_ids = edge_dst[0]
    src_match = (src_ids[:, None] == entity_cols[None, :]).astype(jnp.bfloat16)
    dst_match = (dst_ids[:, None] == entity_cols[None, :]).astype(jnp.bfloat16)
    src_rows = (
        jnp.dot(src_match, emb_bf, preferred_element_type=jnp.float32)
        .astype(jnp.bfloat16)
        .reshape(req_count, group_size, feature_count)
    )
    dst_rows = jnp.dot(dst_match, dst_block, preferred_element_type=jnp.float32).astype(jnp.bfloat16)
    transformed = jnp.einsum(
        "ked,kgd->kge", my_ops, src_rows, preferred_element_type=jnp.float32
    ).reshape(edge_count, feature_count)
    trans_bf = transformed.astype(jnp.bfloat16)
    positive = jnp.sum(transformed * dst_rows.astype(jnp.float32), axis=1)
    pos_grad = -jax.nn.sigmoid(-positive)
    neg_scale = 1.0 / jnp.sqrt(jnp.float32(neg_count))
    block_terms = [pos_grad[:, None] * transformed]
    pieces = []
    for span_id in range(span_count):
        neg_match = (negatives[0, span_id][:, None] == entity_cols[None, :]).astype(jnp.bfloat16)
        neg_rows = jnp.dot(neg_match, dst_block, preferred_element_type=jnp.float32).astype(
            jnp.bfloat16
        )
        edge_rows = trans_bf[span_id * span_size : (span_id + 1) * span_size]
        scores = jnp.dot(edge_rows, neg_rows.T, preferred_element_type=jnp.float32)
        weights = (jax.nn.sigmoid(scores) * neg_scale).astype(jnp.bfloat16)
        pieces.append(jnp.dot(weights, neg_rows, preferred_element_type=jnp.float32))
        block_terms.append(jnp.dot(weights.T, edge_rows, preferred_element_type=jnp.float32))
    g_trans = pos_grad[:, None] * dst_rows.astype(jnp.float32) + jnp.concatenate(pieces, axis=0)
    g_bf = g_trans.astype(jnp.bfloat16).reshape(req_count, group_size, feature_count)

    def slot_grads(index, valid):
        live = valid.astype(jnp.bfloat16)[:, None, None]
        picked = jnp.take(g_bf, jnp.maximum(index, 0), axis=0) * live
        rows = jnp.take(src_rows, jnp.maximum(index, 0), axis=0)
        return jnp.einsum(
            "kge,kgd->ked", picked, rows, preferred_element_type=jnp.float32
        ).reshape(index.shape[0], flat_size)

    src_terms = jnp.einsum(
        "ked,kge->kgd", my_ops, g_bf, preferred_element_type=jnp.float32
    ).reshape(edge_count, feature_count)
    riders = (src_terms, block_terms, src_ids, dst_ids, negatives[0])
    blk_count = lax.axis_size("blk")
    share_size = op_state.shape[1]
    rel_cols = jnp.arange(rel_local, dtype=jnp.int32)
    if rel_count == 2:
        partner_slots = req_of_slot.reshape(rel_count, capacity)
        partner_valid = slot_valid.reshape(rel_count, capacity)
        to_partner = slot_grads(
            lax.dynamic_index_in_dim(partner_slots, 1 - rel_me, 0, keepdims=False),
            lax.dynamic_index_in_dim(partner_valid, 1 - rel_me, 0, keepdims=False),
        )
        from_partner = flipped(to_partner, "rel", 0)
        mine_hit = (owner_ids == rel_me)[:, None] & (local_ids[:, None] == rel_cols[None, :])
        own_dense = slot_grads(
            jnp.sum(jnp.where(mine_hit, jnp.arange(req_count, dtype=jnp.int32)[:, None], 0), axis=0),
            jnp.any(mine_hit, axis=0),
        )
        their_hit = partner_asks[:, None] == rel_cols[None, :]
        their_index = jnp.sum(
            jnp.where(their_hit, jnp.arange(capacity, dtype=jnp.int32)[:, None], 0), axis=0
        )
        their_valid = jnp.any(their_hit, axis=0)
        summed, riders = owner_sum(
            own_dense + pick_rows(from_partner, their_index, their_valid), "blk", riders
        )
    else:
        outgoing = slot_grads(req_of_slot, slot_valid).reshape(
            rel_count, capacity, flat_size
        )
        incoming = exchange(outgoing, "rel").reshape(slot_count, flat_size)
        owner_match = (asked_flat[:, None] == rel_cols[None, :]).astype(jnp.float32)
        summed, riders = owner_sum(scatter_rows(owner_match, incoming), "blk", riders)
    src_terms, block_terms, src_late, dst_late, neg_late = riders
    src_grad = scatter_rows((src_late[:, None] == entity_cols[None, :]).astype(jnp.float32), src_terms)
    block_grad = scatter_rows(
        (dst_late[:, None] == entity_cols[None, :]).astype(jnp.float32), block_terms[0]
    )
    for span_id in range(span_count):
        neg_hit = (neg_late[span_id][:, None] == entity_cols[None, :]).astype(jnp.float32)
        block_grad = block_grad + scatter_rows(neg_hit, block_terms[span_id + 1])
    returned = shifted(block_grad, "blk", -1)
    entity_grad = src_grad + returned
    new_emb_state = emb_state + jnp.mean(entity_grad * entity_grad, axis=1)
    new_emb = embeddings - 0.3 * entity_grad / (jnp.sqrt(new_emb_state)[:, None] + 1e-10)
    op_share = lax.dynamic_index_in_dim(
        operators.reshape(rel_local, blk_count, share_size), lax.axis_index("blk"), 1, keepdims=False
    )
    state_next = op_state + summed * summed
    updated = op_share - 0.3 * summed / (jnp.sqrt(state_next) + 1e-10)
    new_ops = owner_gather(updated, "blk")
    return (
        new_emb,
        new_emb_state,
        new_ops.reshape(rel_local, feature_count, feature_count),
        state_next,
    )


def solution(mesh):
    placed = (
        P(("blk", "rel"), None),
        P(("blk", "rel")),
        P("rel", None, None),
        P("rel", "blk"),
        P(("blk", "rel"), None),
        P(("blk", "rel"), None),
        P(("blk", "rel"), None),
        P(("blk", "rel"), None, None),
    )
    return jax.shard_map(
        shards,
        mesh=mesh,
        in_specs=placed,
        out_specs=(
            P(("blk", "rel"), None),
            P(("blk", "rel")),
            P("rel", None, None),
            P("rel", "blk"),
        ),
        check_vma=False,
    )
```

```python
import jax
import jax.numpy as jnp
from jax import lax
from jax.sharding import PartitionSpec as P


def shifted(value, axis, by):
    count = lax.axis_size(axis)
    return lax.ppermute(value, axis, [(i, (i + by) % count) for i in range(count)])


def flipped(value, axis, bit):
    count = lax.axis_size(axis)
    return lax.ppermute(value, axis, [(i, i ^ (1 << bit)) for i in range(count)])


def chip_hop(value, axis, offset):
    count = lax.axis_size(axis)
    chips = count // 2
    return lax.ppermute(
        value, axis, [(i, ((i // 2 + offset) % chips) * 2 + i % 2) for i in range(count)]
    )


def exchange(rows, axis):
    return lax.all_to_all(rows, axis, split_axis=0, concat_axis=0, tiled=True)


def scatter_rows(onehot, values):
    return lax.dot_general(
        onehot,
        values,
        (((0,), (0,)), ((), ())),
        precision=lax.Precision.HIGHEST,
        preferred_element_type=jnp.float32,
    )


def pick_rows(slots, index, valid):
    picked = jnp.take(slots, jnp.maximum(index, 0), axis=0)
    return jnp.where(valid.reshape((-1,) + (1,) * (slots.ndim - 1)), picked, 0.0)


def owner_sum(own_dense, axis, riders):
    count = lax.axis_size(axis)
    chips = count // 2
    me = lax.axis_index(axis)
    core = me % 2
    chip = me // 2
    height, width = own_dense.shape
    share = width // count
    cur = own_dense.reshape(height, chips, 2, share)
    keep = lax.dynamic_index_in_dim(cur, core, 2, keepdims=False)
    send = lax.dynamic_index_in_dim(cur, 1 - core, 2, keepdims=False)
    got = flipped(send, axis, 0)
    half, riders = lax.optimization_barrier((keep + got, riders))
    total = lax.dynamic_index_in_dim(half, chip, 1, keepdims=False)
    for offset in range(1, chips):
        part = lax.dynamic_index_in_dim(half, (chip + offset) % chips, 1, keepdims=False)
        total = total + chip_hop(part, axis, offset)
    return total, riders


def owner_gather(share_rows, axis):
    count = lax.axis_size(axis)
    chips = count // 2
    me = lax.axis_index(axis)
    core = me % 2
    chip = me // 2
    height, share = share_rows.shape
    pieces = [share_rows]
    for offset in range(1, chips):
        pieces.append(chip_hop(share_rows, axis, chips - offset))
    stacked = jnp.stack(pieces, axis=1)
    order = (jnp.arange(chips, dtype=jnp.int32) - chip) % chips
    mine = jnp.take(stacked, order, axis=1)
    theirs = flipped(mine, axis, 0)
    low = core == 0
    full = jnp.stack([jnp.where(low, mine, theirs), jnp.where(low, theirs, mine)], axis=2)
    return full.reshape(height, count * share)


def shards(embeddings, emb_state, operators, op_state, requests, edge_src, edge_dst, negatives):
    rel_count = lax.axis_size("rel")
    ent_rows, feature_count = embeddings.shape
    rel_local = operators.shape[0]
    req_count = requests.shape[1]
    capacity = max(req_count // 4, req_count // rel_count)
    slot_count = rel_count * capacity
    edge_count = edge_src.shape[1]
    group_size = edge_count // req_count
    span_count = negatives.shape[1]
    neg_count = negatives.shape[2]
    span_size = edge_count // span_count
    flat_size = feature_count * feature_count
    emb_bf = embeddings.astype(jnp.bfloat16)
    dst_block = shifted(emb_bf, "blk", 1)
    request_ids = requests[0]
    owner_ids = request_ids // rel_local
    local_ids = request_ids % rel_local
    owner_hot = (owner_ids[:, None] == jnp.arange(rel_count, dtype=jnp.int32)[None, :]).astype(
        jnp.int32
    )
    rank_ids = jnp.sum((jnp.cumsum(owner_hot, axis=0) - 1) * owner_hot, axis=1)
    slot_of = owner_ids * capacity + rank_ids
    slot_hit = slot_of[:, None] == jnp.arange(slot_count, dtype=jnp.int32)[None, :]
    slot_valid = jnp.any(slot_hit, axis=0)
    req_of_slot = jnp.sum(
        jnp.where(slot_hit, jnp.arange(req_count, dtype=jnp.int32)[:, None], 0), axis=0
    )
    wanted = jnp.where(slot_valid, jnp.take(local_ids, req_of_slot), -1).reshape(
        rel_count, capacity
    )
    op_bf = operators.astype(jnp.bfloat16)
    rel_me = lax.axis_index("rel")
    if rel_count == 2:
        partner_asks = flipped(lax.dynamic_index_in_dim(wanted, 1 - rel_me, 0, keepdims=False), "rel", 0)
        own_asks = lax.dynamic_index_in_dim(wanted, rel_me, 0, keepdims=False)
        served = jnp.take(op_bf, jnp.maximum(partner_asks, 0), axis=0)
        got_ops = flipped(served, "rel", 0)
        own_ops = jnp.take(op_bf, jnp.maximum(own_asks, 0), axis=0)
        both_ops = jnp.concatenate([own_ops, got_ops], axis=0)
        my_ops = jnp.take(both_ops, jnp.where(owner_ids == rel_me, 0, capacity) + rank_ids, axis=0)
    else:
        asked = exchange(wanted, "rel")
        asked_flat = asked.reshape(-1)
        served = jnp.take(op_bf, jnp.maximum(asked_flat, 0), axis=0).reshape(
            rel_count, capacity, feature_count, feature_count
        )
        fetched = exchange(served, "rel").reshape(slot_count, feature_count, feature_count)
        my_ops = jnp.take(fetched, slot_of, axis=0)
    entity_cols = jnp.arange(ent_rows, dtype=jnp.int32)
    src_ids = edge_src[0]
    dst_ids = edge_dst[0]
    src_match = (src_ids[:, None] == entity_cols[None, :]).astype(jnp.bfloat16)
    dst_match = (dst_ids[:, None] == entity_cols[None, :]).astype(jnp.bfloat16)
    src_rows = (
        jnp.dot(src_match, emb_bf, preferred_element_type=jnp.float32)
        .astype(jnp.bfloat16)
        .reshape(req_count, group_size, feature_count)
    )
    dst_rows = jnp.dot(dst_match, dst_block, preferred_element_type=jnp.float32).astype(jnp.bfloat16)
    transformed = jnp.einsum(
        "ked,kgd->kge", my_ops, src_rows, preferred_element_type=jnp.float32
    ).reshape(edge_count, feature_count)
    trans_bf = transformed.astype(jnp.bfloat16)
    positive = jnp.sum(transformed * dst_rows.astype(jnp.float32), axis=1)
    pos_grad = -jax.nn.sigmoid(-positive)
    neg_scale = 1.0 / jnp.sqrt(jnp.float32(neg_count))
    block_terms = [pos_grad[:, None] * transformed]
    pieces = []
    for span_id in range(span_count):
        neg_match = (negatives[0, span_id][:, None] == entity_cols[None, :]).astype(jnp.bfloat16)
        neg_rows = jnp.dot(neg_match, dst_block, preferred_element_type=jnp.float32).astype(
            jnp.bfloat16
        )
        edge_rows = trans_bf[span_id * span_size : (span_id + 1) * span_size]
        scores = jnp.dot(edge_rows, neg_rows.T, preferred_element_type=jnp.float32)
        weights = (jax.nn.sigmoid(scores) * neg_scale).astype(jnp.bfloat16)
        pieces.append(jnp.dot(weights, neg_rows, preferred_element_type=jnp.float32))
        block_terms.append(jnp.dot(weights.T, edge_rows, preferred_element_type=jnp.float32))
    g_trans = pos_grad[:, None] * dst_rows.astype(jnp.float32) + jnp.concatenate(pieces, axis=0)
    g_bf = g_trans.astype(jnp.bfloat16).reshape(req_count, group_size, feature_count)

    def slot_grads(index, valid):
        live = valid.astype(jnp.bfloat16)[:, None, None]
        picked = jnp.take(g_bf, jnp.maximum(index, 0), axis=0) * live
        rows = jnp.take(src_rows, jnp.maximum(index, 0), axis=0)
        return jnp.einsum(
            "kge,kgd->ked", picked, rows, preferred_element_type=jnp.float32
        ).reshape(index.shape[0], flat_size)

    src_terms = jnp.einsum(
        "ked,kge->kgd", my_ops, g_bf, preferred_element_type=jnp.float32
    ).reshape(edge_count, feature_count)
    riders = (src_terms, block_terms, src_ids, dst_ids, negatives[0])
    blk_count = lax.axis_size("blk")
    share_size = op_state.shape[1]
    rel_cols = jnp.arange(rel_local, dtype=jnp.int32)
    if rel_count == 2:
        partner_slots = req_of_slot.reshape(rel_count, capacity)
        partner_valid = slot_valid.reshape(rel_count, capacity)
        to_partner = slot_grads(
            lax.dynamic_index_in_dim(partner_slots, 1 - rel_me, 0, keepdims=False),
            lax.dynamic_index_in_dim(partner_valid, 1 - rel_me, 0, keepdims=False),
        )
        from_partner = flipped(to_partner, "rel", 0)
        mine_hit = (owner_ids == rel_me)[:, None] & (local_ids[:, None] == rel_cols[None, :])
        own_dense = slot_grads(
            jnp.sum(jnp.where(mine_hit, jnp.arange(req_count, dtype=jnp.int32)[:, None], 0), axis=0),
            jnp.any(mine_hit, axis=0),
        )
        their_hit = partner_asks[:, None] == rel_cols[None, :]
        their_index = jnp.sum(
            jnp.where(their_hit, jnp.arange(capacity, dtype=jnp.int32)[:, None], 0), axis=0
        )
        their_valid = jnp.any(their_hit, axis=0)
        summed, riders = owner_sum(
            own_dense + pick_rows(from_partner, their_index, their_valid), "blk", riders
        )
    else:
        outgoing = slot_grads(req_of_slot, slot_valid).reshape(
            rel_count, capacity, flat_size
        )
        incoming = exchange(outgoing, "rel").reshape(slot_count, flat_size)
        owner_match = (asked_flat[:, None] == rel_cols[None, :]).astype(jnp.float32)
        summed, riders = owner_sum(scatter_rows(owner_match, incoming), "blk", riders)
    src_terms, block_terms, src_late, dst_late, neg_late = riders
    src_grad = scatter_rows((src_late[:, None] == entity_cols[None, :]).astype(jnp.float32), src_terms)
    block_grad = scatter_rows(
        (dst_late[:, None] == entity_cols[None, :]).astype(jnp.float32), block_terms[0]
    )
    for span_id in range(span_count):
        neg_hit = (neg_late[span_id][:, None] == entity_cols[None, :]).astype(jnp.float32)
        block_grad = block_grad + scatter_rows(neg_hit, block_terms[span_id + 1])
    op_share = lax.dynamic_index_in_dim(
        operators.reshape(rel_local, blk_count, share_size), lax.axis_index("blk"), 1, keepdims=False
    )
    state_next = op_state + summed * summed
    updated = op_share - 0.3 * summed / (jnp.sqrt(state_next) + 1e-10)
    updated, src_grad, block_grad = lax.optimization_barrier((updated, src_grad, block_grad))
    returned = shifted(block_grad, "blk", -1)
    new_ops = owner_gather(updated, "blk")
    entity_grad = src_grad + returned
    new_emb_state = emb_state + jnp.mean(entity_grad * entity_grad, axis=1)
    new_emb = embeddings - 0.3 * entity_grad / (jnp.sqrt(new_emb_state)[:, None] + 1e-10)
    return (
        new_emb,
        new_emb_state,
        new_ops.reshape(rel_local, feature_count, feature_count),
        state_next,
    )


def solution(mesh):
    placed = (
        P(("blk", "rel"), None),
        P(("blk", "rel")),
        P("rel", None, None),
        P("rel", "blk"),
        P(("blk", "rel"), None),
        P(("blk", "rel"), None),
        P(("blk", "rel"), None),
        P(("blk", "rel"), None, None),
    )
    return jax.shard_map(
        shards,
        mesh=mesh,
        in_specs=placed,
        out_specs=(
            P(("blk", "rel"), None),
            P(("blk", "rel")),
            P("rel", None, None),
            P("rel", "blk"),
        ),
        check_vma=False,
    )
```

```python
import jax
import jax.numpy as jnp
from jax import lax
from jax.sharding import PartitionSpec as P


def shifted(value, axis, by):
    count = lax.axis_size(axis)
    return lax.ppermute(value, axis, [(i, (i + by) % count) for i in range(count)])


def flipped(value, axis, bit):
    count = lax.axis_size(axis)
    return lax.ppermute(value, axis, [(i, i ^ (1 << bit)) for i in range(count)])


def chip_hop(value, axis, offset):
    count = lax.axis_size(axis)
    chips = count // 2
    return lax.ppermute(
        value, axis, [(i, ((i // 2 + offset) % chips) * 2 + i % 2) for i in range(count)]
    )


def exchange(rows, axis):
    return lax.all_to_all(rows, axis, split_axis=0, concat_axis=0, tiled=True)


def scatter_rows(onehot, values):
    return lax.dot_general(
        onehot,
        values,
        (((0,), (0,)), ((), ())),
        precision=lax.Precision.HIGHEST,
        preferred_element_type=jnp.float32,
    )


def pick_rows(slots, index, valid):
    picked = jnp.take(slots, jnp.maximum(index, 0), axis=0)
    return jnp.where(valid.reshape((-1,) + (1,) * (slots.ndim - 1)), picked, 0.0)


def owner_sum(own_dense, axis, riders):
    count = lax.axis_size(axis)
    chips = count // 2
    me = lax.axis_index(axis)
    core = me % 2
    chip = me // 2
    height, width = own_dense.shape
    share = width // count
    cur = own_dense.reshape(height, chips, 2, share)
    keep = lax.dynamic_index_in_dim(cur, core, 2, keepdims=False)
    send = lax.dynamic_index_in_dim(cur, 1 - core, 2, keepdims=False)
    got = flipped(send, axis, 0)
    half, riders = lax.optimization_barrier((keep + got, riders))
    total = lax.dynamic_index_in_dim(half, chip, 1, keepdims=False)
    for offset in range(1, chips):
        part = lax.dynamic_index_in_dim(half, (chip + offset) % chips, 1, keepdims=False)
        total = total + chip_hop(part, axis, offset)
    return total, riders


def owner_gather(share_rows, axis):
    count = lax.axis_size(axis)
    chips = count // 2
    me = lax.axis_index(axis)
    core = me % 2
    chip = me // 2
    height, share = share_rows.shape
    pieces = [share_rows]
    for offset in range(1, chips):
        pieces.append(chip_hop(share_rows, axis, chips - offset))
    stacked = jnp.stack(pieces, axis=1)
    order = (jnp.arange(chips, dtype=jnp.int32) - chip) % chips
    mine = jnp.take(stacked, order, axis=1)
    theirs = flipped(mine, axis, 0)
    low = core == 0
    full = jnp.stack([jnp.where(low, mine, theirs), jnp.where(low, theirs, mine)], axis=2)
    return full.reshape(height, count * share)


def share_of(operators, count, share, index):
    rows, height, width = operators.shape
    starts = [(i * share) // width for i in range(count)]
    span = max(-(-((i * share) - starts[i] * width + share) // width) for i in range(count))
    if any(starts[i] + span > height for i in range(count)):
        return lax.dynamic_index_in_dim(
            operators.reshape(rows, count, share), index, 1, keepdims=False
        )
    first = (index * share) // width
    block = lax.dynamic_slice_in_dim(operators, first, span, 1).reshape(rows, span * width)
    return lax.dynamic_slice_in_dim(block, index * share - first * width, share, 1)


def shards(embeddings, emb_state, operators, op_state, requests, edge_src, edge_dst, negatives):
    rel_count = lax.axis_size("rel")
    ent_rows, feature_count = embeddings.shape
    rel_local = operators.shape[0]
    req_count = requests.shape[1]
    capacity = max(req_count // 4, req_count // rel_count)
    slot_count = rel_count * capacity
    edge_count = edge_src.shape[1]
    group_size = edge_count // req_count
    span_count = negatives.shape[1]
    neg_count = negatives.shape[2]
    span_size = edge_count // span_count
    flat_size = feature_count * feature_count
    emb_bf = embeddings.astype(jnp.bfloat16)
    dst_block = shifted(emb_bf, "blk", 1)
    request_ids = requests[0]
    owner_ids = request_ids // rel_local
    local_ids = request_ids % rel_local
    owner_hot = (owner_ids[:, None] == jnp.arange(rel_count, dtype=jnp.int32)[None, :]).astype(
        jnp.int32
    )
    rank_ids = jnp.sum((jnp.cumsum(owner_hot, axis=0) - 1) * owner_hot, axis=1)
    slot_of = owner_ids * capacity + rank_ids
    slot_hit = slot_of[:, None] == jnp.arange(slot_count, dtype=jnp.int32)[None, :]
    slot_valid = jnp.any(slot_hit, axis=0)
    req_of_slot = jnp.sum(
        jnp.where(slot_hit, jnp.arange(req_count, dtype=jnp.int32)[:, None], 0), axis=0
    )
    wanted = jnp.where(slot_valid, jnp.take(local_ids, req_of_slot), -1).reshape(
        rel_count, capacity
    )
    op_bf = operators.astype(jnp.bfloat16)
    rel_me = lax.axis_index("rel")
    if rel_count == 2:
        partner_asks = flipped(lax.dynamic_index_in_dim(wanted, 1 - rel_me, 0, keepdims=False), "rel", 0)
        own_asks = lax.dynamic_index_in_dim(wanted, rel_me, 0, keepdims=False)
        served = jnp.take(op_bf, jnp.maximum(partner_asks, 0), axis=0)
        got_ops = flipped(served, "rel", 0)
        own_ops = jnp.take(op_bf, jnp.maximum(own_asks, 0), axis=0)
        both_ops = jnp.concatenate([own_ops, got_ops], axis=0)
        my_ops = jnp.take(both_ops, jnp.where(owner_ids == rel_me, 0, capacity) + rank_ids, axis=0)
    else:
        asked = exchange(wanted, "rel")
        asked_flat = asked.reshape(-1)
        served = jnp.take(op_bf, jnp.maximum(asked_flat, 0), axis=0).reshape(
            rel_count, capacity, feature_count, feature_count
        )
        fetched = exchange(served, "rel").reshape(slot_count, feature_count, feature_count)
        my_ops = jnp.take(fetched, slot_of, axis=0)
    entity_cols = jnp.arange(ent_rows, dtype=jnp.int32)
    src_ids = edge_src[0]
    dst_ids = edge_dst[0]
    src_match = (src_ids[:, None] == entity_cols[None, :]).astype(jnp.bfloat16)
    dst_match = (dst_ids[:, None] == entity_cols[None, :]).astype(jnp.bfloat16)
    src_rows = (
        jnp.dot(src_match, emb_bf, preferred_element_type=jnp.float32)
        .astype(jnp.bfloat16)
        .reshape(req_count, group_size, feature_count)
    )
    dst_rows = jnp.dot(dst_match, dst_block, preferred_element_type=jnp.float32).astype(jnp.bfloat16)
    neg_blocks = []
    for span_id in range(span_count):
        neg_match = (negatives[0, span_id][:, None] == entity_cols[None, :]).astype(jnp.bfloat16)
        neg_blocks.append(
            jnp.dot(neg_match, dst_block, preferred_element_type=jnp.float32).astype(jnp.bfloat16)
        )
    my_ops, dst_rows, src_rows, neg_blocks = lax.optimization_barrier(
        (my_ops, dst_rows, src_rows, neg_blocks)
    )
    transformed = jnp.einsum(
        "ked,kgd->kge", my_ops, src_rows, preferred_element_type=jnp.float32
    ).reshape(edge_count, feature_count)
    trans_bf = transformed.astype(jnp.bfloat16)
    positive = jnp.sum(transformed * dst_rows.astype(jnp.float32), axis=1)
    pos_grad = -jax.nn.sigmoid(-positive)
    neg_scale = 1.0 / jnp.sqrt(jnp.float32(neg_count))
    block_terms = [pos_grad[:, None] * transformed]
    pieces = []
    for span_id in range(span_count):
        neg_rows = neg_blocks[span_id]
        edge_rows = trans_bf[span_id * span_size : (span_id + 1) * span_size]
        scores = jnp.dot(edge_rows, neg_rows.T, preferred_element_type=jnp.float32)
        weights = (jax.nn.sigmoid(scores) * neg_scale).astype(jnp.bfloat16)
        pieces.append(jnp.dot(weights, neg_rows, preferred_element_type=jnp.float32))
        block_terms.append(jnp.dot(weights.T, edge_rows, preferred_element_type=jnp.float32))
    g_trans = pos_grad[:, None] * dst_rows.astype(jnp.float32) + jnp.concatenate(pieces, axis=0)
    g_bf = g_trans.astype(jnp.bfloat16).reshape(req_count, group_size, feature_count)

    def slot_grads(index, valid):
        live = valid.astype(jnp.bfloat16)[:, None, None]
        picked = jnp.take(g_bf, jnp.maximum(index, 0), axis=0) * live
        rows = jnp.take(src_rows, jnp.maximum(index, 0), axis=0)
        return jnp.einsum(
            "kge,kgd->ked", picked, rows, preferred_element_type=jnp.float32
        ).reshape(index.shape[0], flat_size)

    src_terms = jnp.einsum(
        "ked,kge->kgd", my_ops, g_bf, preferred_element_type=jnp.float32
    ).reshape(edge_count, feature_count)
    riders = (src_terms, block_terms, src_ids, dst_ids, negatives[0])
    blk_count = lax.axis_size("blk")
    share_size = op_state.shape[1]
    rel_cols = jnp.arange(rel_local, dtype=jnp.int32)
    if rel_count == 2:
        partner_slots = req_of_slot.reshape(rel_count, capacity)
        partner_valid = slot_valid.reshape(rel_count, capacity)
        to_partner = slot_grads(
            lax.dynamic_index_in_dim(partner_slots, 1 - rel_me, 0, keepdims=False),
            lax.dynamic_index_in_dim(partner_valid, 1 - rel_me, 0, keepdims=False),
        )
        from_partner = flipped(to_partner, "rel", 0)
        mine_hit = (owner_ids == rel_me)[:, None] & (local_ids[:, None] == rel_cols[None, :])
        own_dense = slot_grads(
            jnp.sum(jnp.where(mine_hit, jnp.arange(req_count, dtype=jnp.int32)[:, None], 0), axis=0),
            jnp.any(mine_hit, axis=0),
        )
        their_hit = partner_asks[:, None] == rel_cols[None, :]
        their_index = jnp.sum(
            jnp.where(their_hit, jnp.arange(capacity, dtype=jnp.int32)[:, None], 0), axis=0
        )
        their_valid = jnp.any(their_hit, axis=0)
        summed, riders = owner_sum(
            own_dense + pick_rows(from_partner, their_index, their_valid), "blk", riders
        )
    else:
        outgoing = slot_grads(req_of_slot, slot_valid).reshape(
            rel_count, capacity, flat_size
        )
        incoming = exchange(outgoing, "rel").reshape(slot_count, flat_size)
        owner_match = (asked_flat[:, None] == rel_cols[None, :]).astype(jnp.float32)
        summed, riders = owner_sum(scatter_rows(owner_match, incoming), "blk", riders)
    src_terms, block_terms, src_late, dst_late, neg_late = riders
    src_grad = scatter_rows((src_late[:, None] == entity_cols[None, :]).astype(jnp.float32), src_terms)
    block_grad = scatter_rows(
        (dst_late[:, None] == entity_cols[None, :]).astype(jnp.float32), block_terms[0]
    )
    for span_id in range(span_count):
        neg_hit = (neg_late[span_id][:, None] == entity_cols[None, :]).astype(jnp.float32)
        block_grad = block_grad + scatter_rows(neg_hit, block_terms[span_id + 1])
    op_share = share_of(operators, blk_count, share_size, lax.axis_index("blk"))
    state_next = op_state + summed * summed
    updated = op_share - 0.3 * summed / (jnp.sqrt(state_next) + 1e-10)
    updated, src_grad, block_grad = lax.optimization_barrier((updated, src_grad, block_grad))
    returned = shifted(block_grad, "blk", -1)
    new_ops = owner_gather(updated, "blk")
    entity_grad = src_grad + returned
    new_emb_state = emb_state + jnp.mean(entity_grad * entity_grad, axis=1)
    new_emb = embeddings - 0.3 * entity_grad / (jnp.sqrt(new_emb_state)[:, None] + 1e-10)
    return (
        new_emb,
        new_emb_state,
        new_ops.reshape(rel_local, feature_count, feature_count),
        state_next,
    )


def solution(mesh):
    placed = (
        P(("blk", "rel"), None),
        P(("blk", "rel")),
        P("rel", None, None),
        P("rel", "blk"),
        P(("blk", "rel"), None),
        P(("blk", "rel"), None),
        P(("blk", "rel"), None),
        P(("blk", "rel"), None, None),
    )
    return jax.shard_map(
        shards,
        mesh=mesh,
        in_specs=placed,
        out_specs=(
            P(("blk", "rel"), None),
            P(("blk", "rel")),
            P("rel", None, None),
            P("rel", "blk"),
        ),
        check_vma=False,
    )
```

```python
import jax
import jax.numpy as jnp
from jax import lax
from jax.sharding import PartitionSpec as P


def shifted(value, axis, by):
    count = lax.axis_size(axis)
    return lax.ppermute(value, axis, [(i, (i + by) % count) for i in range(count)])


def flipped(value, axis, bit):
    count = lax.axis_size(axis)
    return lax.ppermute(value, axis, [(i, i ^ (1 << bit)) for i in range(count)])


def chip_hop(value, axis, offset):
    count = lax.axis_size(axis)
    chips = count // 2
    return lax.ppermute(
        value, axis, [(i, ((i // 2 + offset) % chips) * 2 + i % 2) for i in range(count)]
    )


def exchange(rows, axis):
    return lax.all_to_all(rows, axis, split_axis=0, concat_axis=0, tiled=True)


def scatter_rows(onehot, values):
    return lax.dot_general(
        onehot,
        values,
        (((0,), (0,)), ((), ())),
        precision=lax.Precision.HIGHEST,
        preferred_element_type=jnp.float32,
    )


def pick_rows(slots, index, valid):
    picked = jnp.take(slots, jnp.maximum(index, 0), axis=0)
    return jnp.where(valid.reshape((-1,) + (1,) * (slots.ndim - 1)), picked, 0.0)


def owner_sum(own_dense, axis, riders):
    count = lax.axis_size(axis)
    chips = count // 2
    me = lax.axis_index(axis)
    core = me % 2
    chip = me // 2
    height, width = own_dense.shape
    share = width // count
    cur = own_dense.reshape(height, chips, 2, share)
    keep = lax.dynamic_index_in_dim(cur, core, 2, keepdims=False)
    send = lax.dynamic_index_in_dim(cur, 1 - core, 2, keepdims=False)
    got = flipped(send, axis, 0)
    half, riders = lax.optimization_barrier((keep + got, riders))
    total = lax.dynamic_index_in_dim(half, chip, 1, keepdims=False)
    for offset in range(1, chips):
        part = lax.dynamic_index_in_dim(half, (chip + offset) % chips, 1, keepdims=False)
        total = total + chip_hop(part, axis, offset)
    return total, riders


def owner_gather(share_rows, axis):
    count = lax.axis_size(axis)
    chips = count // 2
    me = lax.axis_index(axis)
    core = me % 2
    chip = me // 2
    height, share = share_rows.shape
    pieces = [share_rows]
    for offset in range(1, chips):
        pieces.append(chip_hop(share_rows, axis, chips - offset))
    stacked = jnp.stack(pieces, axis=1)
    order = (jnp.arange(chips, dtype=jnp.int32) - chip) % chips
    mine = jnp.take(stacked, order, axis=1)
    theirs = flipped(mine, axis, 0)
    low = core == 0
    full = jnp.stack([jnp.where(low, mine, theirs), jnp.where(low, theirs, mine)], axis=2)
    return full.reshape(height, count * share)


def share_of(operators, count, share, index):
    rows, height, width = operators.shape
    starts = [(i * share) // width for i in range(count)]
    span = max(-(-((i * share) - starts[i] * width + share) // width) for i in range(count))
    if any(starts[i] + span > height for i in range(count)):
        return lax.dynamic_index_in_dim(
            operators.reshape(rows, count, share), index, 1, keepdims=False
        )
    first = (index * share) // width
    block = lax.dynamic_slice_in_dim(operators, first, span, 1).reshape(rows, span * width)
    return lax.dynamic_slice_in_dim(block, index * share - first * width, share, 1)


def shards(embeddings, emb_state, operators, op_state, requests, edge_src, edge_dst, negatives):
    rel_count = lax.axis_size("rel")
    ent_rows, feature_count = embeddings.shape
    rel_local = operators.shape[0]
    req_count = requests.shape[1]
    capacity = max(req_count // 4, req_count // rel_count)
    slot_count = rel_count * capacity
    edge_count = edge_src.shape[1]
    group_size = edge_count // req_count
    span_count = negatives.shape[1]
    neg_count = negatives.shape[2]
    span_size = edge_count // span_count
    flat_size = feature_count * feature_count
    emb_bf = embeddings.astype(jnp.bfloat16)
    dst_block = shifted(emb_bf, "blk", 1)
    request_ids = requests[0]
    owner_ids = request_ids // rel_local
    local_ids = request_ids % rel_local
    owner_hot = (owner_ids[:, None] == jnp.arange(rel_count, dtype=jnp.int32)[None, :]).astype(
        jnp.int32
    )
    rank_ids = jnp.sum((jnp.cumsum(owner_hot, axis=0) - 1) * owner_hot, axis=1)
    slot_of = owner_ids * capacity + rank_ids
    slot_hit = slot_of[:, None] == jnp.arange(slot_count, dtype=jnp.int32)[None, :]
    slot_valid = jnp.any(slot_hit, axis=0)
    req_of_slot = jnp.sum(
        jnp.where(slot_hit, jnp.arange(req_count, dtype=jnp.int32)[:, None], 0), axis=0
    )
    wanted = jnp.where(slot_valid, jnp.take(local_ids, req_of_slot), -1).reshape(
        rel_count, capacity
    )
    op_bf = operators.astype(jnp.bfloat16)
    rel_me = lax.axis_index("rel")
    if rel_count == 2:
        partner_asks = flipped(lax.dynamic_index_in_dim(wanted, 1 - rel_me, 0, keepdims=False), "rel", 0)
        own_asks = lax.dynamic_index_in_dim(wanted, rel_me, 0, keepdims=False)
        served = jnp.take(op_bf, jnp.maximum(partner_asks, 0), axis=0)
        got_ops = flipped(served, "rel", 0)
        own_ops = jnp.take(op_bf, jnp.maximum(own_asks, 0), axis=0)
        both_ops = jnp.concatenate([own_ops, got_ops], axis=0)
        my_ops = jnp.take(both_ops, jnp.where(owner_ids == rel_me, 0, capacity) + rank_ids, axis=0)
    else:
        asked = exchange(wanted, "rel")
        asked_flat = asked.reshape(-1)
        served = jnp.take(op_bf, jnp.maximum(asked_flat, 0), axis=0).reshape(
            rel_count, capacity, feature_count, feature_count
        )
        fetched = exchange(served, "rel").reshape(slot_count, feature_count, feature_count)
        my_ops = jnp.take(fetched, slot_of, axis=0)
    entity_cols = jnp.arange(ent_rows, dtype=jnp.int32)
    src_ids = edge_src[0]
    dst_ids = edge_dst[0]
    src_match = (src_ids[:, None] == entity_cols[None, :]).astype(jnp.bfloat16)
    dst_match = (dst_ids[:, None] == entity_cols[None, :]).astype(jnp.bfloat16)
    src_rows = (
        jnp.dot(src_match, emb_bf, preferred_element_type=jnp.float32)
        .astype(jnp.bfloat16)
        .reshape(req_count, group_size, feature_count)
    )
    dst_rows = jnp.dot(dst_match, dst_block, preferred_element_type=jnp.float32).astype(jnp.bfloat16)
    neg_flat = negatives[0].reshape(span_count * neg_count)
    neg_match = (neg_flat[:, None] == entity_cols[None, :]).astype(jnp.bfloat16)
    neg_all = jnp.dot(neg_match, dst_block, preferred_element_type=jnp.float32).astype(jnp.bfloat16)
    my_ops, dst_rows, src_rows, neg_all = lax.optimization_barrier(
        (my_ops, dst_rows, src_rows, neg_all)
    )
    transformed = jnp.einsum(
        "ked,kgd->kge", my_ops, src_rows, preferred_element_type=jnp.float32
    ).reshape(edge_count, feature_count)
    trans_bf = transformed.astype(jnp.bfloat16)
    positive = jnp.sum(transformed * dst_rows.astype(jnp.float32), axis=1)
    pos_grad = -jax.nn.sigmoid(-positive)
    neg_scale = 1.0 / jnp.sqrt(jnp.float32(neg_count))
    block_terms = [pos_grad[:, None] * transformed]
    neg_spans = neg_all.reshape(span_count, neg_count, feature_count)
    edge_spans = trans_bf.reshape(span_count, span_size, feature_count)
    scores = jnp.einsum("sed,snd->sen", edge_spans, neg_spans, preferred_element_type=jnp.float32)
    weights = (jax.nn.sigmoid(scores) * neg_scale).astype(jnp.bfloat16)
    pieces = jnp.einsum("sen,snd->sed", weights, neg_spans, preferred_element_type=jnp.float32)
    block_terms.append(
        jnp.einsum("sen,sed->snd", weights, edge_spans, preferred_element_type=jnp.float32).reshape(
            span_count * neg_count, feature_count
        )
    )
    g_trans = pos_grad[:, None] * dst_rows.astype(jnp.float32) + pieces.reshape(edge_count, feature_count)
    g_bf = g_trans.astype(jnp.bfloat16).reshape(req_count, group_size, feature_count)

    def slot_grads(index, valid):
        live = valid.astype(jnp.bfloat16)[:, None, None]
        picked = jnp.take(g_bf, jnp.maximum(index, 0), axis=0) * live
        rows = jnp.take(src_rows, jnp.maximum(index, 0), axis=0)
        return jnp.einsum(
            "kge,kgd->ked", picked, rows, preferred_element_type=jnp.float32
        ).reshape(index.shape[0], flat_size)

    src_terms = jnp.einsum(
        "ked,kge->kgd", my_ops, g_bf, preferred_element_type=jnp.float32
    ).reshape(edge_count, feature_count)
    riders = (src_terms, block_terms, src_ids, dst_ids, negatives[0])
    blk_count = lax.axis_size("blk")
    share_size = op_state.shape[1]
    rel_cols = jnp.arange(rel_local, dtype=jnp.int32)
    if rel_count == 2:
        partner_slots = req_of_slot.reshape(rel_count, capacity)
        partner_valid = slot_valid.reshape(rel_count, capacity)
        to_partner = slot_grads(
            lax.dynamic_index_in_dim(partner_slots, 1 - rel_me, 0, keepdims=False),
            lax.dynamic_index_in_dim(partner_valid, 1 - rel_me, 0, keepdims=False),
        )
        from_partner = flipped(to_partner, "rel", 0)
        mine_hit = (owner_ids == rel_me)[:, None] & (local_ids[:, None] == rel_cols[None, :])
        own_dense = slot_grads(
            jnp.sum(jnp.where(mine_hit, jnp.arange(req_count, dtype=jnp.int32)[:, None], 0), axis=0),
            jnp.any(mine_hit, axis=0),
        )
        their_hit = partner_asks[:, None] == rel_cols[None, :]
        their_index = jnp.sum(
            jnp.where(their_hit, jnp.arange(capacity, dtype=jnp.int32)[:, None], 0), axis=0
        )
        their_valid = jnp.any(their_hit, axis=0)
        summed, riders = owner_sum(
            own_dense + pick_rows(from_partner, their_index, their_valid), "blk", riders
        )
    else:
        outgoing = slot_grads(req_of_slot, slot_valid).reshape(
            rel_count, capacity, flat_size
        )
        incoming = exchange(outgoing, "rel").reshape(slot_count, flat_size)
        owner_match = (asked_flat[:, None] == rel_cols[None, :]).astype(jnp.float32)
        summed, riders = owner_sum(scatter_rows(owner_match, incoming), "blk", riders)
    src_terms, block_terms, src_late, dst_late, neg_late = riders
    src_grad = scatter_rows((src_late[:, None] == entity_cols[None, :]).astype(jnp.float32), src_terms)
    block_ids = jnp.concatenate([dst_late, neg_late.reshape(-1)], axis=0)
    block_grad = scatter_rows(
        (block_ids[:, None] == entity_cols[None, :]).astype(jnp.float32),
        jnp.concatenate(block_terms, axis=0),
    )
    op_share = share_of(operators, blk_count, share_size, lax.axis_index("blk"))
    state_next = op_state + summed * summed
    updated = op_share - 0.3 * summed / (jnp.sqrt(state_next) + 1e-10)
    updated, src_grad, block_grad = lax.optimization_barrier((updated, src_grad, block_grad))
    returned = shifted(block_grad, "blk", -1)
    new_ops = owner_gather(updated, "blk")
    entity_grad = src_grad + returned
    new_emb_state = emb_state + jnp.mean(entity_grad * entity_grad, axis=1)
    new_emb = embeddings - 0.3 * entity_grad / (jnp.sqrt(new_emb_state)[:, None] + 1e-10)
    return (
        new_emb,
        new_emb_state,
        new_ops.reshape(rel_local, feature_count, feature_count),
        state_next,
    )


def solution(mesh):
    placed = (
        P(("blk", "rel"), None),
        P(("blk", "rel")),
        P("rel", None, None),
        P("rel", "blk"),
        P(("blk", "rel"), None),
        P(("blk", "rel"), None),
        P(("blk", "rel"), None),
        P(("blk", "rel"), None, None),
    )

    return jax.shard_map(
        shards,
        mesh=mesh,
        in_specs=placed,
        out_specs=(
            P(("blk", "rel"), None),
            P(("blk", "rel")),
            P("rel", None, None),
            P("rel", "blk"),
        ),
        check_vma=False,
    )
```

```python
import jax
import jax.numpy as jnp
from jax import lax
from jax.sharding import PartitionSpec as P


def shifted(value, axis, by):
    count = lax.axis_size(axis)
    return lax.ppermute(value, axis, [(i, (i + by) % count) for i in range(count)])


def flipped(value, axis, bit):
    count = lax.axis_size(axis)
    return lax.ppermute(value, axis, [(i, i ^ (1 << bit)) for i in range(count)])


def chip_hop(value, axis, offset):
    count = lax.axis_size(axis)
    chips = count // 2
    return lax.ppermute(
        value, axis, [(i, ((i // 2 + offset) % chips) * 2 + i % 2) for i in range(count)]
    )


def exchange(rows, axis):
    return lax.all_to_all(rows, axis, split_axis=0, concat_axis=0, tiled=True)


def scatter_rows(onehot, values):
    return lax.dot_general(
        onehot,
        values,
        (((0,), (0,)), ((), ())),
        precision=lax.Precision.HIGHEST,
        preferred_element_type=jnp.float32,
    )


def pick_rows(slots, index, valid):
    picked = jnp.take(slots, jnp.maximum(index, 0), axis=0)
    return jnp.where(valid.reshape((-1,) + (1,) * (slots.ndim - 1)), picked, 0.0)


def owner_sum(own_dense, axis, riders):
    count = lax.axis_size(axis)
    chips = count // 2
    me = lax.axis_index(axis)
    core = me % 2
    chip = me // 2
    height, width = own_dense.shape
    share = width // count
    cur = own_dense.reshape(height, chips, 2, share)
    keep = lax.dynamic_index_in_dim(cur, core, 2, keepdims=False)
    send = lax.dynamic_index_in_dim(cur, 1 - core, 2, keepdims=False)
    got = flipped(send, axis, 0)
    half, riders = lax.optimization_barrier((keep + got, riders))
    total = lax.dynamic_index_in_dim(half, chip, 1, keepdims=False)
    for offset in range(1, chips):
        part = lax.dynamic_index_in_dim(half, (chip + offset) % chips, 1, keepdims=False)
        total = total + chip_hop(part, axis, offset)
    return total, riders


def owner_gather(share_rows, axis):
    count = lax.axis_size(axis)
    chips = count // 2
    me = lax.axis_index(axis)
    core = me % 2
    chip = me // 2
    height, share = share_rows.shape
    pieces = [share_rows]
    for offset in range(1, chips):
        pieces.append(chip_hop(share_rows, axis, chips - offset))
    stacked = jnp.stack(pieces, axis=1)
    order = (jnp.arange(chips, dtype=jnp.int32) - chip) % chips
    mine = jnp.take(stacked, order, axis=1)
    theirs = flipped(mine, axis, 0)
    low = core == 0
    full = jnp.stack([jnp.where(low, mine, theirs), jnp.where(low, theirs, mine)], axis=2)
    return full.reshape(height, count * share)


def share_of(operators, count, share, index):
    rows, height, width = operators.shape
    starts = [(i * share) // width for i in range(count)]
    span = max(-(-((i * share) - starts[i] * width + share) // width) for i in range(count))
    if any(starts[i] + span > height for i in range(count)):
        return lax.dynamic_index_in_dim(
            operators.reshape(rows, count, share), index, 1, keepdims=False
        )
    first = (index * share) // width
    block = lax.dynamic_slice_in_dim(operators, first, span, 1).reshape(rows, span * width)
    return lax.dynamic_slice_in_dim(block, index * share - first * width, share, 1)


def shards(embeddings, emb_state, operators, op_state, requests, edge_src, edge_dst, negatives):
    rel_count = lax.axis_size("rel")
    ent_rows, feature_count = embeddings.shape
    rel_local = operators.shape[0]
    req_count = requests.shape[1]
    capacity = max(req_count // 4, req_count // rel_count)
    slot_count = rel_count * capacity
    edge_count = edge_src.shape[1]
    group_size = edge_count // req_count
    span_count = negatives.shape[1]
    neg_count = negatives.shape[2]
    span_size = edge_count // span_count
    flat_size = feature_count * feature_count
    emb_bf = embeddings.astype(jnp.bfloat16)
    dst_block = shifted(emb_bf, "blk", 1)
    request_ids = requests[0]
    owner_ids = request_ids // rel_local
    local_ids = request_ids % rel_local
    owner_hot = (owner_ids[:, None] == jnp.arange(rel_count, dtype=jnp.int32)[None, :]).astype(
        jnp.int32
    )
    rank_ids = jnp.sum((jnp.cumsum(owner_hot, axis=0) - 1) * owner_hot, axis=1)
    slot_of = owner_ids * capacity + rank_ids
    slot_hit = slot_of[:, None] == jnp.arange(slot_count, dtype=jnp.int32)[None, :]
    slot_valid = jnp.any(slot_hit, axis=0)
    req_of_slot = jnp.sum(
        jnp.where(slot_hit, jnp.arange(req_count, dtype=jnp.int32)[:, None], 0), axis=0
    )
    wanted = jnp.where(slot_valid, jnp.take(local_ids, req_of_slot), -1).reshape(
        rel_count, capacity
    )
    op_bf = operators.astype(jnp.bfloat16)
    rel_me = lax.axis_index("rel")
    if rel_count == 2:
        partner_asks = flipped(
            lax.dynamic_index_in_dim(wanted, 1 - rel_me, 0, keepdims=False), "rel", 0
        )
        own_asks = lax.dynamic_index_in_dim(wanted, rel_me, 0, keepdims=False)
        served = jnp.take(op_bf, jnp.maximum(partner_asks, 0), axis=0)
        got_ops = flipped(served, "rel", 0)
        own_ops = jnp.take(op_bf, jnp.maximum(own_asks, 0), axis=0)
        both_ops = jnp.concatenate([own_ops, got_ops], axis=0)
        my_ops = jnp.take(both_ops, jnp.where(owner_ids == rel_me, 0, capacity) + rank_ids, axis=0)
    else:
        asked = exchange(wanted, "rel")
        asked_flat = asked.reshape(-1)
        served = jnp.take(op_bf, jnp.maximum(asked_flat, 0), axis=0).reshape(
            rel_count, capacity, feature_count, feature_count
        )
        fetched = exchange(served, "rel").reshape(slot_count, feature_count, feature_count)
        my_ops = jnp.take(fetched, slot_of, axis=0)
    entity_cols = jnp.arange(ent_rows, dtype=jnp.int32)
    src_ids = edge_src[0]
    dst_ids = edge_dst[0]
    src_match = (src_ids[:, None] == entity_cols[None, :]).astype(jnp.bfloat16)
    dst_match = (dst_ids[:, None] == entity_cols[None, :]).astype(jnp.bfloat16)
    src_rows = (
        jnp.dot(src_match, emb_bf, preferred_element_type=jnp.float32)
        .astype(jnp.bfloat16)
        .reshape(req_count, group_size, feature_count)
    )
    dst_rows = jnp.dot(dst_match, dst_block, preferred_element_type=jnp.float32).astype(jnp.bfloat16)
    neg_flat = negatives[0].reshape(span_count * neg_count)
    neg_match = (neg_flat[:, None] == entity_cols[None, :]).astype(jnp.bfloat16)
    neg_all = jnp.dot(neg_match, dst_block, preferred_element_type=jnp.float32).astype(jnp.bfloat16)
    my_ops, dst_rows, src_rows, neg_all = lax.optimization_barrier(
        (my_ops, dst_rows, src_rows, neg_all)
    )
    transformed = jnp.einsum(
        "ked,kgd->kge", my_ops, src_rows, preferred_element_type=jnp.float32
    ).reshape(edge_count, feature_count)
    trans_bf = transformed.astype(jnp.bfloat16)
    positive = jnp.sum(transformed * dst_rows.astype(jnp.float32), axis=1)
    pos_grad = -jax.nn.sigmoid(-positive)
    neg_scale = 1.0 / jnp.sqrt(jnp.float32(neg_count))
    block_terms = [pos_grad[:, None] * transformed]
    neg_spans = neg_all.reshape(span_count, neg_count, feature_count)
    edge_spans = trans_bf.reshape(span_count, span_size, feature_count)
    scores = jnp.einsum("sed,snd->sen", edge_spans, neg_spans, preferred_element_type=jnp.float32)
    weights = (jax.nn.sigmoid(scores) * neg_scale).astype(jnp.bfloat16)
    pieces = jnp.einsum("sen,snd->sed", weights, neg_spans, preferred_element_type=jnp.float32)
    block_terms.append(
        jnp.einsum("sen,sed->snd", weights, edge_spans, preferred_element_type=jnp.float32).reshape(
            span_count * neg_count, feature_count
        )
    )
    g_trans = pos_grad[:, None] * dst_rows.astype(jnp.float32) + pieces.reshape(edge_count, feature_count)
    g_bf = g_trans.astype(jnp.bfloat16).reshape(req_count, group_size, feature_count)

    def slot_grads(index, valid):
        live = valid.astype(jnp.bfloat16)[:, None, None]
        picked = jnp.take(g_bf, jnp.maximum(index, 0), axis=0) * live
        rows = jnp.take(src_rows, jnp.maximum(index, 0), axis=0)
        return jnp.einsum(
            "kge,kgd->ked", picked, rows, preferred_element_type=jnp.float32
        ).reshape(index.shape[0], flat_size)

    src_terms = jnp.einsum(
        "ked,kge->kgd", my_ops, g_bf, preferred_element_type=jnp.float32
    ).reshape(edge_count, feature_count)
    riders = (src_terms, block_terms, src_ids, dst_ids, negatives[0])
    blk_count = lax.axis_size("blk")
    share_size = op_state.shape[1]
    rel_cols = jnp.arange(rel_local, dtype=jnp.int32)
    if rel_count == 2:
        partner_slots = req_of_slot.reshape(rel_count, capacity)
        partner_valid = slot_valid.reshape(rel_count, capacity)
        to_partner = slot_grads(
            lax.dynamic_index_in_dim(partner_slots, 1 - rel_me, 0, keepdims=False),
            lax.dynamic_index_in_dim(partner_valid, 1 - rel_me, 0, keepdims=False),
        )
        from_partner = flipped(to_partner, "rel", 0)
        mine_hit = (owner_ids == rel_me)[:, None] & (local_ids[:, None] == rel_cols[None, :])
        own_dense = slot_grads(
            jnp.sum(jnp.where(mine_hit, jnp.arange(req_count, dtype=jnp.int32)[:, None], 0), axis=0),
            jnp.any(mine_hit, axis=0),
        )
        their_hit = partner_asks[:, None] == rel_cols[None, :]
        their_index = jnp.sum(
            jnp.where(their_hit, jnp.arange(capacity, dtype=jnp.int32)[:, None], 0), axis=0
        )
        their_valid = jnp.any(their_hit, axis=0)
        summed, riders = owner_sum(
            own_dense + pick_rows(from_partner, their_index, their_valid), "blk", riders
        )
    else:
        outgoing = slot_grads(req_of_slot, slot_valid).reshape(
            rel_count, capacity, flat_size
        )
        incoming = exchange(outgoing, "rel").reshape(slot_count, flat_size)
        owner_match = (asked_flat[:, None] == rel_cols[None, :]).astype(jnp.float32)
        summed, riders = owner_sum(scatter_rows(owner_match, incoming), "blk", riders)
    src_terms, block_terms, src_late, dst_late, neg_late = riders
    src_grad = lax.optimization_barrier(
        scatter_rows((src_late[:, None] == entity_cols[None, :]).astype(jnp.float32), src_terms)
    )
    block_ids = jnp.concatenate([dst_late, neg_late.reshape(-1)], axis=0)
    block_grad = scatter_rows(
        (block_ids[:, None] == entity_cols[None, :]).astype(jnp.float32),
        jnp.concatenate(block_terms, axis=0),
    )
    op_share = share_of(operators, blk_count, share_size, lax.axis_index("blk"))
    state_next = op_state + summed * summed
    updated = op_share - 0.3 * summed / (jnp.sqrt(state_next) + 1e-10)
    updated, block_grad = lax.optimization_barrier((updated, block_grad))
    returned = shifted(block_grad, "blk", -1)
    new_ops = owner_gather(updated, "blk")
    entity_grad = src_grad + returned
    new_emb_state = emb_state + jnp.mean(entity_grad * entity_grad, axis=1)
    new_emb = embeddings - 0.3 * entity_grad / (jnp.sqrt(new_emb_state)[:, None] + 1e-10)
    return (
        new_emb,
        new_emb_state,
        new_ops.reshape(rel_local, feature_count, feature_count),
        state_next,
    )


def solution(mesh):
    placed = (
        P(("blk", "rel"), None),
        P(("blk", "rel")),
        P("rel", None, None),
        P("rel", "blk"),
        P(("blk", "rel"), None),
        P(("blk", "rel"), None),
        P(("blk", "rel"), None),
        P(("blk", "rel"), None, None),
    )

    return jax.shard_map(
        shards,
        mesh=mesh,
        in_specs=placed,
        out_specs=(
            P(("blk", "rel"), None),
            P(("blk", "rel")),
            P("rel", None, None),
            P("rel", "blk"),
        ),
        check_vma=False,
    )
```

```python
import jax
import jax.numpy as jnp
from jax import lax
from jax.sharding import PartitionSpec as P


def shifted(value, axis, by):
    count = lax.axis_size(axis)
    return lax.ppermute(value, axis, [(i, (i + by) % count) for i in range(count)])


def flipped(value, axis, bit):
    count = lax.axis_size(axis)
    return lax.ppermute(value, axis, [(i, i ^ (1 << bit)) for i in range(count)])


def chip_hop(value, axis, offset):
    count = lax.axis_size(axis)
    chips = count // 2
    return lax.ppermute(
        value, axis, [(i, ((i // 2 + offset) % chips) * 2 + i % 2) for i in range(count)]
    )


def exchange(rows, axis):
    return lax.all_to_all(rows, axis, split_axis=0, concat_axis=0, tiled=True)


def scatter_rows(onehot, values):
    return lax.dot_general(
        onehot,
        values,
        (((0,), (0,)), ((), ())),
        precision=lax.Precision.HIGHEST,
        preferred_element_type=jnp.float32,
    )


def pick_rows(slots, index, valid):
    picked = jnp.take(slots, jnp.maximum(index, 0), axis=0)
    return jnp.where(valid.reshape((-1,) + (1,) * (slots.ndim - 1)), picked, 0.0)


def owner_sum(own_dense, axis, riders):
    count = lax.axis_size(axis)
    chips = count // 2
    me = lax.axis_index(axis)
    core = me % 2
    chip = me // 2
    height, width = own_dense.shape
    share = width // count
    cur = own_dense.reshape(height, chips, 2, share)
    keep = lax.dynamic_index_in_dim(cur, core, 2, keepdims=False)
    send = lax.dynamic_index_in_dim(cur, 1 - core, 2, keepdims=False)
    got = flipped(send, axis, 0)
    half, riders = lax.optimization_barrier((keep + got, riders))
    total = lax.dynamic_index_in_dim(half, chip, 1, keepdims=False)
    for offset in range(1, chips):
        part = lax.dynamic_index_in_dim(half, (chip + offset) % chips, 1, keepdims=False)
        total = total + chip_hop(part, axis, offset)
    return total, riders


def owner_gather(share_rows, axis):
    count = lax.axis_size(axis)
    chips = count // 2
    me = lax.axis_index(axis)
    core = me % 2
    chip = me // 2
    pieces = [share_rows]
    for offset in range(1, chips):
        pieces.append(chip_hop(share_rows, axis, chips - offset))
    stacked = jnp.stack(pieces, axis=1)
    order = (jnp.arange(chips, dtype=jnp.int32) - chip) % chips
    mine = jnp.take(stacked, order, axis=1)
    theirs = flipped(mine, axis, 0)
    low = core == 0
    first = jnp.where(low, mine, theirs)
    second = jnp.where(low, theirs, mine)
    parts = []
    for position in range(chips):
        parts.append(first[:, position])
        parts.append(second[:, position])
    return jnp.concatenate(parts, axis=1)


def share_of(operators, count, share, index):
    rows, height, width = operators.shape
    starts = [(i * share) // width for i in range(count)]
    span = max(-(-((i * share) - starts[i] * width + share) // width) for i in range(count))
    if any(starts[i] + span > height for i in range(count)):
        return lax.dynamic_index_in_dim(
            operators.reshape(rows, count, share), index, 1, keepdims=False
        )
    first = (index * share) // width
    block = lax.dynamic_slice_in_dim(operators, first, span, 1).reshape(rows, span * width)
    return lax.dynamic_slice_in_dim(block, index * share - first * width, share, 1)


def shards(embeddings, emb_state, operators, op_state, requests, edge_src, edge_dst, negatives):
    rel_count = lax.axis_size("rel")
    ent_rows, feature_count = embeddings.shape
    rel_local = operators.shape[0]
    req_count = requests.shape[1]
    capacity = max(req_count // 4, req_count // rel_count)
    slot_count = rel_count * capacity
    edge_count = edge_src.shape[1]
    group_size = edge_count // req_count
    span_count = negatives.shape[1]
    neg_count = negatives.shape[2]
    span_size = edge_count // span_count
    flat_size = feature_count * feature_count
    emb_bf = embeddings.astype(jnp.bfloat16)
    dst_block = shifted(emb_bf, "blk", 1)
    request_ids = requests[0]
    owner_ids = request_ids // rel_local
    local_ids = request_ids % rel_local
    owner_hot = (owner_ids[:, None] == jnp.arange(rel_count, dtype=jnp.int32)[None, :]).astype(
        jnp.int32
    )
    rank_ids = jnp.sum((jnp.cumsum(owner_hot, axis=0) - 1) * owner_hot, axis=1)
    slot_of = owner_ids * capacity + rank_ids
    slot_hit = slot_of[:, None] == jnp.arange(slot_count, dtype=jnp.int32)[None, :]
    slot_valid = jnp.any(slot_hit, axis=0)
    req_of_slot = jnp.sum(
        jnp.where(slot_hit, jnp.arange(req_count, dtype=jnp.int32)[:, None], 0), axis=0
    )
    wanted = jnp.where(slot_valid, jnp.take(local_ids, req_of_slot), -1).reshape(
        rel_count, capacity
    )
    op_bf = operators.astype(jnp.bfloat16)
    rel_me = lax.axis_index("rel")
    if rel_count == 2:
        partner_asks = flipped(
            lax.dynamic_index_in_dim(wanted, 1 - rel_me, 0, keepdims=False), "rel", 0
        )
        own_asks = lax.dynamic_index_in_dim(wanted, rel_me, 0, keepdims=False)
        served = jnp.take(op_bf, jnp.maximum(partner_asks, 0), axis=0)
        got_ops = flipped(served, "rel", 0)
        own_ops = jnp.take(op_bf, jnp.maximum(own_asks, 0), axis=0)
        both_ops = jnp.concatenate([own_ops, got_ops], axis=0)
        my_ops = jnp.take(both_ops, jnp.where(owner_ids == rel_me, 0, capacity) + rank_ids, axis=0)
    else:
        asked = exchange(wanted, "rel")
        asked_flat = asked.reshape(-1)
        served = jnp.take(op_bf, jnp.maximum(asked_flat, 0), axis=0).reshape(
            rel_count, capacity, feature_count, feature_count
        )
        fetched = exchange(served, "rel").reshape(slot_count, feature_count, feature_count)
        my_ops = jnp.take(fetched, slot_of, axis=0)
    entity_cols = jnp.arange(ent_rows, dtype=jnp.int32)
    src_ids = edge_src[0]
    dst_ids = edge_dst[0]
    src_match = (src_ids[:, None] == entity_cols[None, :]).astype(jnp.bfloat16)
    dst_match = (dst_ids[:, None] == entity_cols[None, :]).astype(jnp.bfloat16)
    src_rows = (
        jnp.dot(src_match, emb_bf, preferred_element_type=jnp.float32)
        .astype(jnp.bfloat16)
        .reshape(req_count, group_size, feature_count)
    )
    dst_rows = jnp.dot(dst_match, dst_block, preferred_element_type=jnp.float32).astype(jnp.bfloat16)
    neg_flat = negatives[0].reshape(span_count * neg_count)
    neg_match = (neg_flat[:, None] == entity_cols[None, :]).astype(jnp.bfloat16)
    neg_all = jnp.dot(neg_match, dst_block, preferred_element_type=jnp.float32).astype(jnp.bfloat16)
    my_ops, dst_rows, src_rows, neg_all = lax.optimization_barrier(
        (my_ops, dst_rows, src_rows, neg_all)
    )
    transformed = jnp.einsum(
        "ked,kgd->kge", my_ops, src_rows, preferred_element_type=jnp.float32
    ).reshape(edge_count, feature_count)
    trans_bf = transformed.astype(jnp.bfloat16)
    positive = jnp.sum(transformed * dst_rows.astype(jnp.float32), axis=1)
    pos_grad = -jax.nn.sigmoid(-positive)
    neg_scale = 1.0 / jnp.sqrt(jnp.float32(neg_count))
    block_terms = [pos_grad[:, None] * transformed]
    neg_spans = neg_all.reshape(span_count, neg_count, feature_count)
    edge_spans = trans_bf.reshape(span_count, span_size, feature_count)
    scores = jnp.einsum("sed,snd->sen", edge_spans, neg_spans, preferred_element_type=jnp.float32)
    weights = (jax.nn.sigmoid(scores) * neg_scale).astype(jnp.bfloat16)
    pieces = jnp.einsum("sen,snd->sed", weights, neg_spans, preferred_element_type=jnp.float32)
    block_terms.append(
        jnp.einsum("sen,sed->snd", weights, edge_spans, preferred_element_type=jnp.float32).reshape(
            span_count * neg_count, feature_count
        )
    )
    g_trans = pos_grad[:, None] * dst_rows.astype(jnp.float32) + pieces.reshape(edge_count, feature_count)
    g_bf = g_trans.astype(jnp.bfloat16).reshape(req_count, group_size, feature_count)

    def slot_grads(index, valid):
        live = valid.astype(jnp.bfloat16)[:, None, None]
        picked = jnp.take(g_bf, jnp.maximum(index, 0), axis=0) * live
        rows = jnp.take(src_rows, jnp.maximum(index, 0), axis=0)
        return jnp.einsum(
            "kge,kgd->ked", picked, rows, preferred_element_type=jnp.float32
        ).reshape(index.shape[0], flat_size)

    src_terms = jnp.einsum(
        "ked,kge->kgd", my_ops, g_bf, preferred_element_type=jnp.float32
    ).reshape(edge_count, feature_count)
    riders = (src_terms, block_terms, src_ids, dst_ids, negatives[0])
    blk_count = lax.axis_size("blk")
    share_size = op_state.shape[1]
    rel_cols = jnp.arange(rel_local, dtype=jnp.int32)
    if rel_count == 2:
        partner_slots = req_of_slot.reshape(rel_count, capacity)
        partner_valid = slot_valid.reshape(rel_count, capacity)
        to_partner = slot_grads(
            lax.dynamic_index_in_dim(partner_slots, 1 - rel_me, 0, keepdims=False),
            lax.dynamic_index_in_dim(partner_valid, 1 - rel_me, 0, keepdims=False),
        )
        from_partner = flipped(to_partner, "rel", 0)
        mine_hit = (owner_ids == rel_me)[:, None] & (local_ids[:, None] == rel_cols[None, :])
        own_dense = slot_grads(
            jnp.sum(jnp.where(mine_hit, jnp.arange(req_count, dtype=jnp.int32)[:, None], 0), axis=0),
            jnp.any(mine_hit, axis=0),
        )
        their_hit = partner_asks[:, None] == rel_cols[None, :]
        their_index = jnp.sum(
            jnp.where(their_hit, jnp.arange(capacity, dtype=jnp.int32)[:, None], 0), axis=0
        )
        their_valid = jnp.any(their_hit, axis=0)
        summed, riders = owner_sum(
            own_dense + pick_rows(from_partner, their_index, their_valid), "blk", riders
        )
    else:
        outgoing = slot_grads(req_of_slot, slot_valid).reshape(
            rel_count, capacity, flat_size
        )
        incoming = exchange(outgoing, "rel").reshape(slot_count, flat_size)
        owner_match = (asked_flat[:, None] == rel_cols[None, :]).astype(jnp.float32)
        summed, riders = owner_sum(scatter_rows(owner_match, incoming), "blk", riders)
    src_terms, block_terms, src_late, dst_late, neg_late = riders
    src_grad = lax.optimization_barrier(
        scatter_rows((src_late[:, None] == entity_cols[None, :]).astype(jnp.float32), src_terms)
    )
    block_ids = jnp.concatenate([dst_late, neg_late.reshape(-1)], axis=0)
    block_grad = scatter_rows(
        (block_ids[:, None] == entity_cols[None, :]).astype(jnp.float32),
        jnp.concatenate(block_terms, axis=0),
    )
    op_share = share_of(operators, blk_count, share_size, lax.axis_index("blk"))
    state_next = op_state + summed * summed
    updated = op_share - 0.3 * summed / (jnp.sqrt(state_next) + 1e-10)
    updated, block_grad = lax.optimization_barrier((updated, block_grad))
    returned = shifted(block_grad, "blk", -1)
    new_ops = owner_gather(updated, "blk")
    entity_grad = src_grad + returned
    new_emb_state = emb_state + jnp.mean(entity_grad * entity_grad, axis=1)
    new_emb = embeddings - 0.3 * entity_grad / (jnp.sqrt(new_emb_state)[:, None] + 1e-10)
    return (
        new_emb,
        new_emb_state,
        new_ops.reshape(rel_local, feature_count, feature_count),
        state_next,
    )


def solution(mesh):
    placed = (
        P(("blk", "rel"), None),
        P(("blk", "rel")),
        P("rel", None, None),
        P("rel", "blk"),
        P(("blk", "rel"), None),
        P(("blk", "rel"), None),
        P(("blk", "rel"), None),
        P(("blk", "rel"), None, None),
    )

    return jax.shard_map(
        shards,
        mesh=mesh,
        in_specs=placed,
        out_specs=(
            P(("blk", "rel"), None),
            P(("blk", "rel")),
            P("rel", None, None),
            P("rel", "blk"),
        ),
        check_vma=False,
    )
```

```python
import jax
import jax.numpy as jnp
from jax import lax
from jax.sharding import PartitionSpec as P


def shifted(value, axis, by):
    count = lax.axis_size(axis)
    return lax.ppermute(value, axis, [(i, (i + by) % count) for i in range(count)])


def flipped(value, axis, bit):
    count = lax.axis_size(axis)
    return lax.ppermute(value, axis, [(i, i ^ (1 << bit)) for i in range(count)])


def chip_hop(value, axis, offset):
    count = lax.axis_size(axis)
    chips = count // 2
    return lax.ppermute(
        value, axis, [(i, ((i // 2 + offset) % chips) * 2 + i % 2) for i in range(count)]
    )


def exchange(rows, axis):
    return lax.all_to_all(rows, axis, split_axis=0, concat_axis=0, tiled=True)


def scatter_rows(onehot, values):
    return lax.dot_general(
        onehot,
        values,
        (((0,), (0,)), ((), ())),
        precision=lax.Precision.HIGHEST,
        preferred_element_type=jnp.float32,
    )


def pick_rows(slots, index, valid):
    picked = jnp.take(slots, jnp.maximum(index, 0), axis=0)
    return jnp.where(valid.reshape((-1,) + (1,) * (slots.ndim - 1)), picked, 0.0)


def owner_sum(own_dense, axis, riders):
    count = lax.axis_size(axis)
    chips = count // 2
    me = lax.axis_index(axis)
    core = me % 2
    chip = me // 2
    height, width = own_dense.shape
    share = width // count
    cur = own_dense.reshape(height, chips, 2, share)
    keep = lax.dynamic_index_in_dim(cur, core, 2, keepdims=False)
    send = lax.dynamic_index_in_dim(cur, 1 - core, 2, keepdims=False)
    got = flipped(send, axis, 0)
    half, riders = lax.optimization_barrier((keep + got, riders))
    total = lax.dynamic_index_in_dim(half, chip, 1, keepdims=False)
    for offset in range(1, chips):
        part = lax.dynamic_index_in_dim(half, (chip + offset) % chips, 1, keepdims=False)
        total = total + chip_hop(part, axis, offset)
    return total, riders


def owner_gather(share_rows, axis):
    count = lax.axis_size(axis)
    chips = count // 2
    me = lax.axis_index(axis)
    core = me % 2
    chip = me // 2
    height, share = share_rows.shape
    pieces = [share_rows]
    for offset in range(1, chips):
        pieces.append(chip_hop(share_rows, axis, chips - offset))
    stacked = jnp.stack(pieces, axis=1)
    order = (jnp.arange(chips, dtype=jnp.int32) - chip) % chips
    mine = jnp.take(stacked, order, axis=1)
    theirs = flipped(mine, axis, 0)
    low = core == 0
    full = jnp.stack([jnp.where(low, mine, theirs), jnp.where(low, theirs, mine)], axis=2)
    return full.reshape(height, count * share)


def share_of(operators, count, share, index):
    rows, height, width = operators.shape
    starts = [(i * share) // width for i in range(count)]
    span = max(-(-((i * share) - starts[i] * width + share) // width) for i in range(count))
    if any(starts[i] + span > height for i in range(count)):
        return lax.dynamic_index_in_dim(
            operators.reshape(rows, count, share), index, 1, keepdims=False
        )
    first = (index * share) // width
    block = lax.dynamic_slice_in_dim(operators, first, span, 1).reshape(rows, span * width)
    return lax.dynamic_slice_in_dim(block, index * share - first * width, share, 1)


def shards(embeddings, emb_state, operators, op_state, requests, edge_src, edge_dst, negatives):
    rel_count = lax.axis_size("rel")
    ent_rows, feature_count = embeddings.shape
    rel_local = operators.shape[0]
    req_count = requests.shape[1]
    capacity = max(req_count // 4, req_count // rel_count)
    slot_count = rel_count * capacity
    edge_count = edge_src.shape[1]
    group_size = edge_count // req_count
    span_count = negatives.shape[1]
    neg_count = negatives.shape[2]
    span_size = edge_count // span_count
    flat_size = feature_count * feature_count
    emb_bf = embeddings.astype(jnp.bfloat16)
    dst_block = shifted(emb_bf, "blk", 1)
    request_ids = requests[0]
    owner_ids = request_ids // rel_local
    local_ids = request_ids % rel_local
    owner_hot = (owner_ids[:, None] == jnp.arange(rel_count, dtype=jnp.int32)[None, :]).astype(
        jnp.int32
    )
    rank_ids = jnp.sum((jnp.cumsum(owner_hot, axis=0) - 1) * owner_hot, axis=1)
    slot_of = owner_ids * capacity + rank_ids
    slot_hit = slot_of[:, None] == jnp.arange(slot_count, dtype=jnp.int32)[None, :]
    slot_valid = jnp.any(slot_hit, axis=0)
    req_of_slot = jnp.sum(
        jnp.where(slot_hit, jnp.arange(req_count, dtype=jnp.int32)[:, None], 0), axis=0
    )
    wanted = jnp.where(slot_valid, jnp.take(local_ids, req_of_slot), -1).reshape(
        rel_count, capacity
    )
    op_bf = operators.astype(jnp.bfloat16)
    rel_me = lax.axis_index("rel")
    if rel_count == 2:
        partner_asks = flipped(
            lax.dynamic_index_in_dim(wanted, 1 - rel_me, 0, keepdims=False), "rel", 0
        )
        own_asks = lax.dynamic_index_in_dim(wanted, rel_me, 0, keepdims=False)
        served = jnp.take(op_bf, jnp.maximum(partner_asks, 0), axis=0)
        got_ops = flipped(served, "rel", 0)
        own_ops = jnp.take(op_bf, jnp.maximum(own_asks, 0), axis=0)
        both_ops = jnp.concatenate([own_ops, got_ops], axis=0)
        my_ops = jnp.take(both_ops, jnp.where(owner_ids == rel_me, 0, capacity) + rank_ids, axis=0)
    else:
        asked = exchange(wanted, "rel")
        asked_flat = asked.reshape(-1)
        served = jnp.take(op_bf, jnp.maximum(asked_flat, 0), axis=0).reshape(
            rel_count, capacity, feature_count, feature_count
        )
        fetched = exchange(served, "rel").reshape(slot_count, feature_count, feature_count)
        my_ops = jnp.take(fetched, slot_of, axis=0)
    entity_cols = jnp.arange(ent_rows, dtype=jnp.int32)
    src_ids = edge_src[0]
    dst_ids = edge_dst[0]
    src_match = (src_ids[:, None] == entity_cols[None, :]).astype(jnp.bfloat16)
    dst_match = (dst_ids[:, None] == entity_cols[None, :]).astype(jnp.bfloat16)
    src_rows = (
        jnp.dot(src_match, emb_bf, preferred_element_type=jnp.float32)
        .astype(jnp.bfloat16)
        .reshape(req_count, group_size, feature_count)
    )
    dst_rows = jnp.dot(dst_match, dst_block, preferred_element_type=jnp.float32).astype(jnp.bfloat16)
    neg_flat = negatives[0].reshape(span_count * neg_count)
    neg_match = (neg_flat[:, None] == entity_cols[None, :]).astype(jnp.bfloat16)
    neg_all = jnp.dot(neg_match, dst_block, preferred_element_type=jnp.float32).astype(jnp.bfloat16)
    my_ops, dst_rows, src_rows, neg_all = lax.optimization_barrier(
        (my_ops, dst_rows, src_rows, neg_all)
    )
    transformed = jnp.einsum(
        "ked,kgd->kge", my_ops, src_rows, preferred_element_type=jnp.float32
    ).reshape(edge_count, feature_count)
    trans_bf = transformed.astype(jnp.bfloat16)
    positive = jnp.sum(transformed * dst_rows.astype(jnp.float32), axis=1)
    pos_grad = -jax.nn.sigmoid(-positive)
    neg_scale = 1.0 / jnp.sqrt(jnp.float32(neg_count))
    block_terms = [pos_grad[:, None] * transformed]
    neg_spans = neg_all.reshape(span_count, neg_count, feature_count)
    edge_spans = trans_bf.reshape(span_count, span_size, feature_count)
    scores = jnp.einsum("sed,snd->sen", edge_spans, neg_spans, preferred_element_type=jnp.float32)
    weights = (jax.nn.sigmoid(scores) * neg_scale).astype(jnp.bfloat16)
    pieces = jnp.einsum("sen,snd->sed", weights, neg_spans, preferred_element_type=jnp.float32)
    block_terms.append(
        jnp.einsum("sen,sed->snd", weights, edge_spans, preferred_element_type=jnp.float32).reshape(
            span_count * neg_count, feature_count
        )
    )
    g_trans = pos_grad[:, None] * dst_rows.astype(jnp.float32) + pieces.reshape(edge_count, feature_count)
    g_bf = g_trans.astype(jnp.bfloat16).reshape(req_count, group_size, feature_count)

    def slot_grads(index, valid):
        live = valid.astype(jnp.bfloat16)[:, None, None]
        picked = jnp.take(g_bf, jnp.maximum(index, 0), axis=0) * live
        rows = jnp.take(src_rows, jnp.maximum(index, 0), axis=0)
        return jnp.einsum(
            "kge,kgd->ked", picked, rows, preferred_element_type=jnp.float32
        ).reshape(index.shape[0], flat_size)

    src_terms = jnp.einsum(
        "ked,kge->kgd", my_ops, g_bf, preferred_element_type=jnp.float32
    ).reshape(edge_count, feature_count)
    riders = (src_terms, block_terms, src_ids, dst_ids, negatives[0])
    blk_count = lax.axis_size("blk")
    share_size = op_state.shape[1]
    rel_cols = jnp.arange(rel_local, dtype=jnp.int32)
    if rel_count == 2:
        partner_slots = req_of_slot.reshape(rel_count, capacity)
        partner_valid = slot_valid.reshape(rel_count, capacity)
        to_partner = slot_grads(
            lax.dynamic_index_in_dim(partner_slots, 1 - rel_me, 0, keepdims=False),
            lax.dynamic_index_in_dim(partner_valid, 1 - rel_me, 0, keepdims=False),
        )
        from_partner = flipped(to_partner, "rel", 0)
        mine_hit = (owner_ids == rel_me)[:, None] & (local_ids[:, None] == rel_cols[None, :])
        own_dense = slot_grads(
            jnp.sum(jnp.where(mine_hit, jnp.arange(req_count, dtype=jnp.int32)[:, None], 0), axis=0),
            jnp.any(mine_hit, axis=0),
        )
        their_hit = partner_asks[:, None] == rel_cols[None, :]
        their_index = jnp.sum(
            jnp.where(their_hit, jnp.arange(capacity, dtype=jnp.int32)[:, None], 0), axis=0
        )
        their_valid = jnp.any(their_hit, axis=0)
        summed, riders = owner_sum(
            own_dense + pick_rows(from_partner, their_index, their_valid), "blk", riders
        )
    else:
        outgoing = slot_grads(req_of_slot, slot_valid).reshape(
            rel_count, capacity, flat_size
        )
        incoming = exchange(outgoing, "rel").reshape(slot_count, flat_size)
        owner_match = (asked_flat[:, None] == rel_cols[None, :]).astype(jnp.float32)
        summed, riders = owner_sum(scatter_rows(owner_match, incoming), "blk", riders)
    src_terms, block_terms, src_late, dst_late, neg_late = riders
    src_grad = lax.optimization_barrier(
        scatter_rows((src_late[:, None] == entity_cols[None, :]).astype(jnp.float32), src_terms)
    )
    block_ids = jnp.concatenate([dst_late, neg_late.reshape(-1)], axis=0)
    block_vals = jnp.concatenate(block_terms, axis=0)
    half_rows = ent_rows // 2
    block_grad = tuple(
        scatter_rows(
            (block_ids[:, None] == entity_cols[None, h * half_rows : (h + 1) * half_rows]).astype(
                jnp.float32
            ),
            block_vals,
        )
        for h in range(2)
    )
    op_share = share_of(operators, blk_count, share_size, lax.axis_index("blk"))
    state_next = op_state + summed * summed
    updated = op_share - 0.3 * summed / (jnp.sqrt(state_next) + 1e-10)
    updated, block_last = lax.optimization_barrier((updated, block_grad[1]))
    block_grad = (block_grad[0], block_last)
    returned_a = shifted(block_grad[0], "blk", -1)
    returned = jnp.concatenate([returned_a, shifted(block_grad[1], "blk", -1)], axis=0)
    new_ops = owner_gather(updated, "blk")
    entity_grad = src_grad + returned
    new_emb_state = emb_state + jnp.mean(entity_grad * entity_grad, axis=1)
    new_emb = embeddings - 0.3 * entity_grad / (jnp.sqrt(new_emb_state)[:, None] + 1e-10)
    return (
        new_emb,
        new_emb_state,
        new_ops.reshape(rel_local, feature_count, feature_count),
        state_next,
    )


def solution(mesh):
    placed = (
        P(("blk", "rel"), None),
        P(("blk", "rel")),
        P("rel", None, None),
        P("rel", "blk"),
        P(("blk", "rel"), None),
        P(("blk", "rel"), None),
        P(("blk", "rel"), None),
        P(("blk", "rel"), None, None),
    )

    return jax.shard_map(
        shards,
        mesh=mesh,
        in_specs=placed,
        out_specs=(
            P(("blk", "rel"), None),
            P(("blk", "rel")),
            P("rel", None, None),
            P("rel", "blk"),
        ),
        check_vma=False,
    )
```

```python
import jax
import jax.numpy as jnp
from jax import lax
from jax.sharding import PartitionSpec as P


def shifted(value, axis, by):
    count = lax.axis_size(axis)
    return lax.ppermute(value, axis, [(i, (i + by) % count) for i in range(count)])


def flipped(value, axis, bit):
    count = lax.axis_size(axis)
    return lax.ppermute(value, axis, [(i, i ^ (1 << bit)) for i in range(count)])


def chip_hop(value, axis, offset):
    count = lax.axis_size(axis)
    chips = count // 2
    return lax.ppermute(
        value, axis, [(i, ((i // 2 + offset) % chips) * 2 + i % 2) for i in range(count)]
    )


def exchange(rows, axis):
    return lax.all_to_all(rows, axis, split_axis=0, concat_axis=0, tiled=True)


def scatter_rows(onehot, values):
    return lax.dot_general(
        onehot,
        values,
        (((0,), (0,)), ((), ())),
        precision=lax.Precision.HIGHEST,
        preferred_element_type=jnp.float32,
    )


def pick_rows(slots, index, valid):
    picked = jnp.take(slots, jnp.maximum(index, 0), axis=0)
    return jnp.where(valid.reshape((-1,) + (1,) * (slots.ndim - 1)), picked, 0.0)


def owner_sum(own_dense, axis, riders):
    count = lax.axis_size(axis)
    chips = count // 2
    me = lax.axis_index(axis)
    core = me % 2
    chip = me // 2
    height, width = own_dense.shape
    share = width // count
    cur = own_dense.reshape(height, chips, 2, share)
    keep = lax.dynamic_index_in_dim(cur, core, 2, keepdims=False)
    send = lax.dynamic_index_in_dim(cur, 1 - core, 2, keepdims=False)
    got = flipped(send, axis, 0)
    half, riders = lax.optimization_barrier((keep + got, riders))
    total = lax.dynamic_index_in_dim(half, chip, 1, keepdims=False)
    for offset in range(1, chips):
        part = lax.dynamic_index_in_dim(half, (chip + offset) % chips, 1, keepdims=False)
        total = total + chip_hop(part, axis, offset)
    return total, riders


def owner_gather(share_rows, axis):
    count = lax.axis_size(axis)
    chips = count // 2
    me = lax.axis_index(axis)
    core = me % 2
    chip = me // 2
    height, share = share_rows.shape
    pieces = [share_rows]
    for offset in range(1, chips):
        pieces.append(chip_hop(share_rows, axis, chips - offset))
    stacked = jnp.stack(pieces, axis=1)
    order = (jnp.arange(chips, dtype=jnp.int32) - chip) % chips
    mine = jnp.take(stacked, order, axis=1)
    theirs = flipped(mine, axis, 0)
    low = core == 0
    full = jnp.stack([jnp.where(low, mine, theirs), jnp.where(low, theirs, mine)], axis=2)
    return full.reshape(height, count * share)


def share_of(operators, count, share, index):
    rows, height, width = operators.shape
    starts = [(i * share) // width for i in range(count)]
    span = max(-(-((i * share) - starts[i] * width + share) // width) for i in range(count))
    if any(starts[i] + span > height for i in range(count)):
        return lax.dynamic_index_in_dim(
            operators.reshape(rows, count, share), index, 1, keepdims=False
        )
    first = (index * share) // width
    block = lax.dynamic_slice_in_dim(operators, first, span, 1).reshape(rows, span * width)
    return lax.dynamic_slice_in_dim(block, index * share - first * width, share, 1)


def shards(embeddings, emb_state, operators, op_state, requests, edge_src, edge_dst, negatives):
    rel_count = lax.axis_size("rel")
    ent_rows, feature_count = embeddings.shape
    rel_local = operators.shape[0]
    req_count = requests.shape[1]
    capacity = max(req_count // 4, req_count // rel_count)
    slot_count = rel_count * capacity
    edge_count = edge_src.shape[1]
    group_size = edge_count // req_count
    span_count = negatives.shape[1]
    neg_count = negatives.shape[2]
    span_size = edge_count // span_count
    flat_size = feature_count * feature_count
    emb_bf = embeddings.astype(jnp.bfloat16)
    dst_block = shifted(emb_bf, "blk", 1)
    request_ids = requests[0]
    owner_ids = request_ids // rel_local
    local_ids = request_ids % rel_local
    owner_hot = (owner_ids[:, None] == jnp.arange(rel_count, dtype=jnp.int32)[None, :]).astype(
        jnp.int32
    )
    rank_ids = jnp.sum((jnp.cumsum(owner_hot, axis=0) - 1) * owner_hot, axis=1)
    slot_of = owner_ids * capacity + rank_ids
    slot_hit = slot_of[:, None] == jnp.arange(slot_count, dtype=jnp.int32)[None, :]
    slot_valid = jnp.any(slot_hit, axis=0)
    req_of_slot = jnp.sum(
        jnp.where(slot_hit, jnp.arange(req_count, dtype=jnp.int32)[:, None], 0), axis=0
    )
    wanted = jnp.where(slot_valid, jnp.take(local_ids, req_of_slot), -1).reshape(
        rel_count, capacity
    )
    op_bf = operators.astype(jnp.bfloat16)
    rel_me = lax.axis_index("rel")
    if rel_count == 2:
        partner_asks = flipped(
            lax.dynamic_index_in_dim(wanted, 1 - rel_me, 0, keepdims=False), "rel", 0
        )
        own_asks = lax.dynamic_index_in_dim(wanted, rel_me, 0, keepdims=False)
        served = jnp.take(op_bf, jnp.maximum(partner_asks, 0), axis=0)
        got_ops = flipped(served, "rel", 0)
        own_ops = jnp.take(op_bf, jnp.maximum(own_asks, 0), axis=0)
        both_ops = jnp.concatenate([own_ops, got_ops], axis=0)
        my_ops = jnp.take(both_ops, jnp.where(owner_ids == rel_me, 0, capacity) + rank_ids, axis=0)
    else:
        asked = exchange(wanted, "rel")
        asked_flat = asked.reshape(-1)
        served = jnp.take(op_bf, jnp.maximum(asked_flat, 0), axis=0).reshape(
            rel_count, capacity, feature_count, feature_count
        )
        fetched = exchange(served, "rel").reshape(slot_count, feature_count, feature_count)
        my_ops = jnp.take(fetched, slot_of, axis=0)
    entity_cols = jnp.arange(ent_rows, dtype=jnp.int32)
    src_ids = edge_src[0]
    dst_ids = edge_dst[0]
    src_match = (src_ids[:, None] == entity_cols[None, :]).astype(jnp.bfloat16)
    dst_match = (dst_ids[:, None] == entity_cols[None, :]).astype(jnp.bfloat16)
    src_rows = (
        jnp.dot(src_match, emb_bf, preferred_element_type=jnp.float32)
        .astype(jnp.bfloat16)
        .reshape(req_count, group_size, feature_count)
    )
    dst_rows = jnp.dot(dst_match, dst_block, preferred_element_type=jnp.float32).astype(jnp.bfloat16)
    neg_flat = negatives[0].reshape(span_count * neg_count)
    neg_match = (neg_flat[:, None] == entity_cols[None, :]).astype(jnp.bfloat16)
    neg_all = jnp.dot(neg_match, dst_block, preferred_element_type=jnp.float32).astype(jnp.bfloat16)
    my_ops, dst_rows, src_rows, neg_all = lax.optimization_barrier(
        (my_ops, dst_rows, src_rows, neg_all)
    )
    transformed = jnp.einsum(
        "ked,kgd->kge", my_ops, src_rows, preferred_element_type=jnp.float32
    ).reshape(edge_count, feature_count)
    trans_bf = transformed.astype(jnp.bfloat16)
    positive = jnp.sum(transformed * dst_rows.astype(jnp.float32), axis=1)
    pos_grad = -jax.nn.sigmoid(-positive)
    neg_scale = 1.0 / jnp.sqrt(jnp.float32(neg_count))
    block_terms = [pos_grad[:, None] * transformed]
    neg_spans = neg_all.reshape(span_count, neg_count, feature_count)
    edge_spans = trans_bf.reshape(span_count, span_size, feature_count)
    scores = jnp.einsum("sed,snd->sen", edge_spans, neg_spans, preferred_element_type=jnp.float32)
    weights = (jax.nn.sigmoid(scores) * neg_scale).astype(jnp.bfloat16)
    pieces = jnp.einsum("sen,snd->sed", weights, neg_spans, preferred_element_type=jnp.float32)
    block_terms.append(
        jnp.einsum("sen,sed->snd", weights, edge_spans, preferred_element_type=jnp.float32).reshape(
            span_count * neg_count, feature_count
        )
    )
    g_trans = pos_grad[:, None] * dst_rows.astype(jnp.float32) + pieces.reshape(edge_count, feature_count)
    g_bf = g_trans.astype(jnp.bfloat16).reshape(req_count, group_size, feature_count)

    def slot_grads(index, valid):
        live = valid.astype(jnp.bfloat16)[:, None, None]
        picked = jnp.take(g_bf, jnp.maximum(index, 0), axis=0) * live
        rows = jnp.take(src_rows, jnp.maximum(index, 0), axis=0)
        return jnp.einsum(
            "kge,kgd->ked", picked, rows, preferred_element_type=jnp.float32
        ).reshape(index.shape[0], flat_size)

    src_terms = jnp.einsum(
        "ked,kge->kgd", my_ops, g_bf, preferred_element_type=jnp.float32
    ).reshape(edge_count, feature_count)
    riders = (src_terms, block_terms, src_ids, dst_ids, negatives[0])
    blk_count = lax.axis_size("blk")
    share_size = op_state.shape[1]
    rel_cols = jnp.arange(rel_local, dtype=jnp.int32)
    if rel_count == 2:
        partner_slots = req_of_slot.reshape(rel_count, capacity)
        partner_valid = slot_valid.reshape(rel_count, capacity)
        to_partner = slot_grads(
            lax.dynamic_index_in_dim(partner_slots, 1 - rel_me, 0, keepdims=False),
            lax.dynamic_index_in_dim(partner_valid, 1 - rel_me, 0, keepdims=False),
        )
        from_partner = flipped(to_partner, "rel", 0)
        mine_hit = (owner_ids == rel_me)[:, None] & (local_ids[:, None] == rel_cols[None, :])
        own_dense = slot_grads(
            jnp.sum(jnp.where(mine_hit, jnp.arange(req_count, dtype=jnp.int32)[:, None], 0), axis=0),
            jnp.any(mine_hit, axis=0),
        )
        their_hit = partner_asks[:, None] == rel_cols[None, :]
        their_index = jnp.sum(
            jnp.where(their_hit, jnp.arange(capacity, dtype=jnp.int32)[:, None], 0), axis=0
        )
        their_valid = jnp.any(their_hit, axis=0)
        summed, riders = owner_sum(
            own_dense + pick_rows(from_partner, their_index, their_valid), "blk", riders
        )
    else:
        outgoing = slot_grads(req_of_slot, slot_valid).reshape(
            rel_count, capacity, flat_size
        )
        incoming = exchange(outgoing, "rel").reshape(slot_count, flat_size)
        owner_match = (asked_flat[:, None] == rel_cols[None, :]).astype(jnp.float32)
        summed, riders = owner_sum(scatter_rows(owner_match, incoming), "blk", riders)
    src_terms, block_terms, src_late, dst_late, neg_late = riders
    src_grad = lax.optimization_barrier(
        scatter_rows((src_late[:, None] == entity_cols[None, :]).astype(jnp.float32), src_terms)
    )
    block_ids = jnp.concatenate([dst_late, neg_late.reshape(-1)], axis=0)
    block_vals = jnp.concatenate(block_terms, axis=0)
    half_rows = ent_rows // 4
    block_grad = tuple(
        scatter_rows(
            (block_ids[:, None] == entity_cols[None, h * half_rows : (h + 1) * half_rows]).astype(
                jnp.float32
            ),
            block_vals,
        )
        for h in range(4)
    )
    op_share = share_of(operators, blk_count, share_size, lax.axis_index("blk"))
    state_next = op_state + summed * summed
    updated = op_share - 0.3 * summed / (jnp.sqrt(state_next) + 1e-10)
    updated, block_last = lax.optimization_barrier((updated, block_grad[-1]))
    block_grad = block_grad[:-1] + (block_last,)
    returned = jnp.concatenate([shifted(part, "blk", -1) for part in block_grad], axis=0)
    new_ops = owner_gather(updated, "blk")
    entity_grad = src_grad + returned
    new_emb_state = emb_state + jnp.mean(entity_grad * entity_grad, axis=1)
    new_emb = embeddings - 0.3 * entity_grad / (jnp.sqrt(new_emb_state)[:, None] + 1e-10)
    return (
        new_emb,
        new_emb_state,
        new_ops.reshape(rel_local, feature_count, feature_count),
        state_next,
    )


def solution(mesh):
    placed = (
        P(("blk", "rel"), None),
        P(("blk", "rel")),
        P("rel", None, None),
        P("rel", "blk"),
        P(("blk", "rel"), None),
        P(("blk", "rel"), None),
        P(("blk", "rel"), None),
        P(("blk", "rel"), None, None),
    )

    return jax.shard_map(
        shards,
        mesh=mesh,
        in_specs=placed,
        out_specs=(
            P(("blk", "rel"), None),
            P(("blk", "rel")),
            P("rel", None, None),
            P("rel", "blk"),
        ),
        check_vma=False,
    )
```
